768 devices in a mesh: gx: 24 (over y_hi, z), gy: 32 (over x, y_lo, core).
Axes of the slice: x: 4, y: 8 (y_hi: 2, y_lo: 4; y = y_hi * 4 + y_lo), z: 12, core: 2. Of those that a mesh axis runs over, the one named last changes fastest.
Arguments:
- coarse_state: float32 [3, 768, 4096], P(None, 'gx', 'gy'), may hold values from -6 to 6
- refined_box_state: float32 [24, 64, 3, 64, 256], P('gx', 'gy'), may hold values from -6 to 6
- box_parent: int32 [24, 64], replicated, may hold values from 0 to 32, as said below
Outputs:
- coarse_next: float32 [3, 768, 4096], P(None, 'gx', 'gy')
- fine_next: float32 [24, 64, 3, 64, 256], P('gx', 'gy')
The draws below stay inside these ranges and needn't reach their ends.
Inputs may be any that keep to these rules, and one draw needn't show every extreme that they name: `box_parent`: entry k of row a names the block row whose refined box sits in slot k of column a; slot k lies on the device of index k // 2 along gy. No block row is named twice in a row; the named blocks of a row form one cyclic run of 16 to 32 consecutive block rows; the value 32 marks an empty slot.
All inputs are finite; a program needn't handle non-finite values.
Results may differ from the reference program's by a relative error of at most 0.00002.
Values sent between devices are 32-bit elements; how exact they have to be, the bound alone decides.
No kernel may reach another device: no remote copies, remote signals or barrier semaphores. Data moves between devices by JAX's collectives and lax.ppermute only.
A program may use at most 64 MiB of HBM per device.

```python
import jax
import jax.numpy as jnp
from jax import lax

CX = 32
CY = 128
BLOCK_COLUMNS = 24
BLOCKS_Y = 32
BOX_SLOTS = 64
NX = 768
NY = 4096
REFINED_CELLS_X = 64
REFINED_CELLS_Y = 256


def draw_box_parent(key, part):

    def one_column(column_key):
        key_start, key_length, sorted_key_order = jax.random.split(column_key, 3)
        first_block = jax.random.randint(key_start, (), 0, BLOCKS_Y)
        run_length = jax.random.randint(key_length, (), BLOCKS_Y // 2, BLOCKS_Y + 1)
        sort_ordering = jax.random.permutation(sorted_key_order, BOX_SLOTS)
        slot_positions = jnp.arange(BOX_SLOTS, dtype=jnp.int32)
        entry_list = jnp.where(slot_positions < run_length, (first_block + slot_positions) % BLOCKS_Y, BLOCKS_Y).astype(jnp.int32)
        return jnp.zeros((BOX_SLOTS,), jnp.int32).at[sort_ordering].set(entry_list)
    return jax.vmap(one_column)(jax.random.split(key, BLOCK_COLUMNS))


def steps_of(rng, extent, cuts, least, largest):
    def one(position, parts):
        steps = jax.random.uniform(jax.random.fold_in(jax.random.fold_in(rng, 6), position), (parts,), jnp.float32, least / len(cuts), largest / len(cuts))
        return jnp.repeat(jnp.exp(steps), extent[position] // parts).reshape((-1,) + (1,) * (len(extent) - position - 1))

    loudness = one(*cuts[0])
    for cut in cuts[1:]:
        loudness = loudness * one(*cut)
    return loudness


def gaussian(stream_key, extent, spread, bound, cuts=(), held_as=jnp.bfloat16):
    loudness = steps_of(stream_key, extent, cuts, -0.22, 0.18) if cuts else 1.0
    array = jax.random.normal(stream_key, extent, jnp.float32) * spread * loudness
    return jnp.minimum(jnp.maximum(array, -bound), bound).astype(held_as)


def setup_inputs(seed: int = 0) -> dict:
    keys = jax.random.split(jax.random.key(seed), 4)
    return {
        "coarse_state": gaussian(keys[0], (3, NX, NY), 1.0, 6.0, ((1, 24), (2, 32)), jnp.float32),
        "refined_box_state": gaussian(keys[1], (BLOCK_COLUMNS, BOX_SLOTS, 3, REFINED_CELLS_X, REFINED_CELLS_Y), 1.0, 6.0, ((0, 24), (1, 32)), jnp.float32),
        "box_parent": draw_box_parent(jax.random.fold_in(keys[3], 71), 0),
    }


LAM_COARSE = 0.2
LAM_FINE = 0.4


def face_flux_x(padded, span_x, span_y):
    cell_minus = padded[:, 0:span_x + 1, 2:span_y + 2]
    cell_left = padded[:, 1:span_x + 2, 2:span_y + 2]
    cell_right = padded[:, 2:span_x + 3, 2:span_y + 2]
    cell_plus = padded[:, 3:span_x + 4, 2:span_y + 2]
    face_mean = (7.0 * (cell_left + cell_right) - (cell_minus + cell_plus)) / 12.0
    face_jump = cell_right - cell_left
    return jnp.stack([face_mean[1] - 0.5 * face_jump[0], face_mean[0] - 0.5 * face_jump[1], -0.5 * face_jump[2]])


def face_flux_y(padded, span_x, span_y):
    cell_minus = padded[:, 2:span_x + 2, 0:span_y + 1]
    cell_left = padded[:, 2:span_x + 2, 1:span_y + 2]
    cell_right = padded[:, 2:span_x + 2, 2:span_y + 3]
    cell_plus = padded[:, 2:span_x + 2, 3:span_y + 4]
    face_mean = (7.0 * (cell_left + cell_right) - (cell_minus + cell_plus)) / 12.0
    face_jump = cell_right - cell_left
    return jnp.stack([face_mean[2] - 0.5 * face_jump[0], -0.5 * face_jump[1], face_mean[0] - 0.5 * face_jump[2]])


def advance_rate(padded, factor):
    span_x = padded.shape[1] - 4
    span_y = padded.shape[2] - 4
    flux_x = face_flux_x(padded, span_x, span_y)
    flux_y = face_flux_y(padded, span_x, span_y)
    change = -factor * ((flux_x[:, 1:] - flux_x[:, :-1]) + (flux_y[:, :, 1:] - flux_y[:, :, :-1]))
    return change, flux_x, flux_y


def inject_side(coarse_edge):
    doubled = jnp.repeat(coarse_edge, 2, axis=-1)
    return jnp.broadcast_to(doubled[..., None, :], doubled.shape[:-1] + (2, doubled.shape[-1]))


def inject_end(coarse_edge):
    doubled = jnp.repeat(coarse_edge, 2, axis=-1)
    return jnp.broadcast_to(doubled[..., None], doubled.shape + (2,))


def assemble(field, ghost_left, ghost_right, ghost_low, ghost_high):
    middle = jnp.concatenate([ghost_low, field, ghost_high], axis=-1)
    zero_band = jnp.zeros(ghost_left.shape[:-1] + (2,), field.dtype)
    left_full = jnp.concatenate([zero_band, ghost_left, zero_band], axis=-1)
    right_full = jnp.concatenate([zero_band, ghost_right, zero_band], axis=-1)
    return jnp.concatenate([left_full, middle, right_full], axis=-2)


def fine_section(field, ghost_left, ghost_right, ghost_low, ghost_high):
    padded = assemble(field, ghost_left, ghost_right, ghost_low, ghost_high)
    change, flux_x, flux_y = advance_rate(padded, LAM_FINE)
    return change, flux_x[:, 0], flux_x[:, -1], flux_y[:, :, 0], flux_y[:, :, -1]


def pair_mean(values):
    return 0.5 * (values[..., 0::2] + values[..., 1::2])


def restrict(field):
    return 0.25 * ((field[..., 0::2, 0::2] + field[..., 1::2, 0::2]) + (field[..., 0::2, 1::2] + field[..., 1::2, 1::2]))


def to_blocks(field):
    return field.reshape(3, BLOCK_COLUMNS, CX, BLOCKS_Y, CY).transpose(1, 3, 0, 2, 4)


def from_blocks(blocked):
    return blocked.transpose(2, 0, 3, 1, 4).reshape(3, NX, NY)


def home_ghosts(home_field, coarse_now, refined):
    blocked = to_blocks(coarse_now)
    flag_left = jnp.roll(refined, 1, 0)[:, :, None, None, None]
    ghost_left = jnp.where(flag_left, jnp.roll(home_field[:, :, :, -2:, :], 1, 0), inject_side(jnp.roll(blocked[:, :, :, -1, :], 1, 0)))
    flag_right = jnp.roll(refined, -1, 0)[:, :, None, None, None]
    ghost_right = jnp.where(flag_right, jnp.roll(home_field[:, :, :, :2, :], -1, 0), inject_side(jnp.roll(blocked[:, :, :, 0, :], -1, 0)))
    flag_low = jnp.roll(refined, 1, 1)[:, :, None, None, None]
    ghost_low = jnp.where(flag_low, jnp.roll(home_field[..., -2:], 1, 1), inject_end(jnp.roll(blocked[..., -1], 1, 1)))
    flag_high = jnp.roll(refined, -1, 1)[:, :, None, None, None]
    ghost_high = jnp.where(flag_high, jnp.roll(home_field[..., :2], -1, 1), inject_end(jnp.roll(blocked[..., 0], -1, 1)))
    return ghost_left, ghost_right, ghost_low, ghost_high


def reference(coarse_state, refined_box_state, box_parent):
    margin = ((0, 0), (2, 2), (2, 2))
    rate_one, flux_x1, flux_y1 = advance_rate(jnp.pad(coarse_state, margin, mode="wrap"), LAM_COARSE)
    coarse_one = coarse_state + rate_one
    rate_two, flux_x2, flux_y2 = advance_rate(jnp.pad(coarse_one, margin, mode="wrap"), LAM_COARSE)
    coarse_heun = 0.5 * ((coarse_state + coarse_one) + rate_two)
    faces_x = 0.5 * (flux_x1 + flux_x2)
    faces_y = 0.5 * (flux_y1 + flux_y2)

    block_ids = jnp.arange(BLOCKS_Y, dtype=jnp.int32)
    refined = jnp.any(box_parent[:, :, None] == block_ids[None, None, :], axis=1)
    column_ids = jnp.broadcast_to(jnp.arange(BLOCK_COLUMNS, dtype=jnp.int32)[:, None], box_parent.shape)
    home_start = jnp.zeros((BLOCK_COLUMNS, BLOCKS_Y, 3, REFINED_CELLS_X, REFINED_CELLS_Y), refined_box_state.dtype).at[column_ids, box_parent].set(refined_box_state, mode="drop")

    def fine_rates(home_field, coarse_now):
        ghosts = home_ghosts(home_field, coarse_now, refined)
        return lax.map(lambda pieces: jax.vmap(fine_section)(*pieces), (home_field,) + ghosts)

    rate_f1, left_one, right_one, low_one, high_one = fine_rates(home_start, coarse_state)
    home_one = home_start + rate_f1
    rate_f2, left_two, right_two, low_two, high_two = fine_rates(home_one, coarse_one)
    home_final = 0.5 * ((home_start + home_one) + rate_f2)
    reg_left = pair_mean(0.5 * (left_one + left_two))
    reg_right = pair_mean(0.5 * (right_one + right_two))
    reg_low = pair_mean(0.5 * (low_one + low_two))
    reg_high = pair_mean(0.5 * (high_one + high_two))

    face_left = faces_x[:, 0:NX:CX].reshape(3, BLOCK_COLUMNS, BLOCKS_Y, CY).transpose(1, 2, 0, 3)
    face_right = faces_x[:, CX:NX + 1:CX].reshape(3, BLOCK_COLUMNS, BLOCKS_Y, CY).transpose(1, 2, 0, 3)
    face_low = faces_y[:, :, 0:NY:CY].reshape(3, BLOCK_COLUMNS, CX, BLOCKS_Y).transpose(1, 3, 0, 2)
    face_high = faces_y[:, :, CY:NY + 1:CY].reshape(3, BLOCK_COLUMNS, CX, BLOCKS_Y).transpose(1, 3, 0, 2)

    corr_left = jnp.where(jnp.roll(refined, 1, 0)[:, :, None, None], LAM_COARSE * (jnp.roll(reg_right, 1, 0) - face_left), 0.0)
    corr_right = jnp.where(jnp.roll(refined, -1, 0)[:, :, None, None], LAM_COARSE * (face_right - jnp.roll(reg_left, -1, 0)), 0.0)
    corr_low = jnp.where(jnp.roll(refined, 1, 1)[:, :, None, None], LAM_COARSE * (jnp.roll(reg_high, 1, 1) - face_low), 0.0)
    corr_high = jnp.where(jnp.roll(refined, -1, 1)[:, :, None, None], LAM_COARSE * (face_high - jnp.roll(reg_low, -1, 1)), 0.0)
    corr_x = jnp.concatenate([corr_left[:, :, :, None, :], jnp.zeros((BLOCK_COLUMNS, BLOCKS_Y, 3, CX - 2, CY), coarse_state.dtype), corr_right[:, :, :, None, :]], axis=3)
    corr_y = jnp.concatenate([corr_low[..., None], jnp.zeros((BLOCK_COLUMNS, BLOCKS_Y, 3, CX, CY - 2), coarse_state.dtype), corr_high[..., None]], axis=4)
    new_blocks = (to_blocks(coarse_heun) + corr_x) + corr_y
    new_blocks = jnp.where(refined[:, :, None, None, None], restrict(home_final), new_blocks)
    coarse_next = from_blocks(new_blocks)

    is_live = box_parent < BLOCKS_Y
    clipped = jnp.minimum(box_parent, BLOCKS_Y - 1)
    picked = home_final[column_ids, clipped]
    fine_next = jnp.where(is_live[:, :, None, None, None], picked, 0.0)
    return coarse_next, fine_next
```

```python
import jax
import jax.numpy as jnp
from jax import lax
from jax.sharding import PartitionSpec as P

LAM_COARSE = 0.2
LAM_FINE = 0.4


def extended(cells, sides, width):
    for axis, dim in sides:
        count = lax.axis_size(axis)
        head = lax.slice_in_dim(cells, 0, width, axis=dim)
        tail = lax.slice_in_dim(cells, cells.shape[dim] - width, cells.shape[dim], axis=dim)
        cells = jnp.concatenate(
            [
                lax.ppermute(tail, axis, [(i, (i + 1) % count) for i in range(count)]),
                cells,
                lax.ppermute(head, axis, [((i + 1) % count, i) for i in range(count)]),
            ],
            axis=dim,
        )
    return cells


def face_flux_x(padded, span_x, span_y):
    cell_minus = padded[:, 0 : span_x + 1, 2 : span_y + 2]
    cell_left = padded[:, 1 : span_x + 2, 2 : span_y + 2]
    cell_right = padded[:, 2 : span_x + 3, 2 : span_y + 2]
    cell_plus = padded[:, 3 : span_x + 4, 2 : span_y + 2]
    face_mean = (7.0 * (cell_left + cell_right) - (cell_minus + cell_plus)) / 12.0
    face_jump = cell_right - cell_left
    return jnp.stack(
        [face_mean[1] - 0.5 * face_jump[0], face_mean[0] - 0.5 * face_jump[1], -0.5 * face_jump[2]]
    )


def face_flux_y(padded, span_x, span_y):
    cell_minus = padded[:, 2 : span_x + 2, 0 : span_y + 1]
    cell_left = padded[:, 2 : span_x + 2, 1 : span_y + 2]
    cell_right = padded[:, 2 : span_x + 2, 2 : span_y + 3]
    cell_plus = padded[:, 2 : span_x + 2, 3 : span_y + 4]
    face_mean = (7.0 * (cell_left + cell_right) - (cell_minus + cell_plus)) / 12.0
    face_jump = cell_right - cell_left
    return jnp.stack(
        [face_mean[2] - 0.5 * face_jump[0], -0.5 * face_jump[1], face_mean[0] - 0.5 * face_jump[2]]
    )


def advance_rate(padded, factor):
    span_x = padded.shape[1] - 4
    span_y = padded.shape[2] - 4
    flux_x = face_flux_x(padded, span_x, span_y)
    flux_y = face_flux_y(padded, span_x, span_y)
    change = -factor * (flux_x[:, 1:] - flux_x[:, :-1] + (flux_y[:, :, 1:] - flux_y[:, :, :-1]))
    return (change, flux_x, flux_y)


def inject_side(coarse_edge):
    doubled = jnp.repeat(coarse_edge, 2, axis=-1)
    return jnp.broadcast_to(doubled[..., None, :], doubled.shape[:-1] + (2, doubled.shape[-1]))


def inject_end(coarse_edge):
    doubled = jnp.repeat(coarse_edge, 2, axis=-1)
    return jnp.broadcast_to(doubled[..., None], doubled.shape + (2,))


def assemble(field, ghost_left, ghost_right, ghost_low, ghost_high):
    middle = jnp.concatenate([ghost_low, field, ghost_high], axis=-1)
    zero_band = jnp.zeros(ghost_left.shape[:-1] + (2,), field.dtype)
    left_full = jnp.concatenate([zero_band, ghost_left, zero_band], axis=-1)
    right_full = jnp.concatenate([zero_band, ghost_right, zero_band], axis=-1)
    return jnp.concatenate([left_full, middle, right_full], axis=-2)


def fine_section(field, ghost_left, ghost_right, ghost_low, ghost_high):
    padded = assemble(field, ghost_left, ghost_right, ghost_low, ghost_high)
    change, flux_x, flux_y = advance_rate(padded, LAM_FINE)
    return (change, flux_x[:, 0], flux_x[:, -1], flux_y[:, :, 0], flux_y[:, :, -1])


def pair_mean(values):
    return 0.5 * (values[..., 0::2] + values[..., 1::2])


def restrict(field):
    return 0.25 * (
        field[..., 0::2, 0::2]
        + field[..., 1::2, 0::2]
        + (field[..., 0::2, 1::2] + field[..., 1::2, 1::2])
    )


def coarse_margin(field):
    return extended(field, (("gx", 1), ("gy", 2)), 2)


def pick_from(row_index, strips, coarse_edges, targets):
    flag, fine_row, fine_sub, edge_row = targets
    sub_index = jnp.arange(strips.shape[1], dtype=jnp.int32)
    hit_mask = (
        (row_index[None, :, None] == fine_row[:, None, None])
        & (sub_index[None, None, :] == fine_sub[:, None, None])
        & flag[:, None, None]
    )
    fine_part = jnp.sum(
        jnp.where(hit_mask[:, :, :, None, None, None], strips[None], 0.0), axis=(1, 2)
    )
    edge_mask = (row_index[None, :] == edge_row[:, None]) & jnp.logical_not(flag)[:, None]
    edge_part = jnp.sum(jnp.where(edge_mask[:, :, None, None], coarse_edges[None], 0.0), axis=1)
    return (fine_part, edge_part)


def gather_rows(parts):
    flat = jnp.concatenate([part.reshape(-1) for part in parts])[None]
    rows = lax.all_gather(flat, "gy", axis=0, tiled=True)
    count = rows.shape[0]
    out = []
    offset = 0
    for part in parts:
        out.append(rows[:, offset : offset + part.size].reshape((count,) + part.shape))
        offset += part.size
    return tuple(out)


def shards(coarse_state, refined_box_state, box_parent):
    count_x = lax.axis_size("gx")
    count_y = lax.axis_size("gy")
    column = lax.axis_index("gx")
    device_row = lax.axis_index("gy")
    slot_count = refined_box_state.shape[1]
    fine_box = refined_box_state[0]
    span_x = coarse_state.shape[1]
    span_y = coarse_state.shape[2]
    block_ids = jnp.arange(count_y, dtype=jnp.int32)
    block_hits = box_parent[:, :, None] == block_ids[None, None, :]
    refined = jnp.any(block_hits, axis=1)
    slot_ids = jnp.arange(box_parent.shape[1], dtype=jnp.int32)
    slot_of = jnp.sum(jnp.where(block_hits, slot_ids[None, :, None], 0), axis=1)
    column_left = (column - 1) % count_x
    column_right = (column + 1) % count_x
    below_block = (device_row - 1) % count_y
    above_block = (device_row + 1) % count_y
    own_table = lax.dynamic_index_in_dim(box_parent, column, 0, keepdims=False)
    left_table = lax.dynamic_index_in_dim(box_parent, column_left, 0, keepdims=False)
    right_table = lax.dynamic_index_in_dim(box_parent, column_right, 0, keepdims=False)
    own_parents = lax.dynamic_slice_in_dim(own_table, device_row * slot_count, slot_count)
    is_live = own_parents < count_y
    parent = jnp.minimum(own_parents, count_y - 1)

    def fine_source(table_column, block):
        flag = refined[table_column, block]
        slot_index = slot_of[table_column, block]
        return (flag, slot_index // slot_count, slot_index % slot_count, block)

    targets_left = fine_source(column_left, parent)
    targets_right = fine_source(column_right, parent)
    targets_low = fine_source(column, (parent - 1) % count_y)
    targets_high = fine_source(column, (parent + 1) % count_y)
    rate_one, flux_x1, flux_y1 = advance_rate(coarse_margin(coarse_state), LAM_COARSE)
    coarse_one = coarse_state + rate_one
    rate_two, flux_x2, flux_y2 = advance_rate(coarse_margin(coarse_one), LAM_COARSE)
    coarse_heun = 0.5 * (coarse_state + coarse_one + rate_two)

    def fine_rates(field, coarse_now):
        strip_left = field[:, :, :2, :]
        strip_right = field[:, :, -2:, :]
        strip_low = field[..., :2]
        strip_high = field[..., -2:]
        edge_left = coarse_now[:, 0, :]
        edge_right = coarse_now[:, -1, :]
        edge_low = coarse_now[:, :, 0]
        edge_high = coarse_now[:, :, -1]
        strip_size = strip_left.size
        edge_size = edge_left.size
        side_pack = jnp.concatenate(
            [
                strip_right.reshape(-1),
                edge_right.reshape(-1),
                strip_left.reshape(-1),
                edge_left.reshape(-1),
            ]
        )[None]
        sides = extended(side_pack, (("gx", 0),), 1)
        from_left = sides[0]
        from_right = sides[2]
        left_strips = from_left[:strip_size].reshape(strip_right.shape)
        left_edges = from_left[strip_size : strip_size + edge_size].reshape(edge_right.shape)
        right_strips = from_right[strip_size + edge_size : 2 * strip_size + edge_size].reshape(
            strip_left.shape
        )
        right_edges = from_right[2 * strip_size + edge_size :].reshape(edge_left.shape)
        pieces = gather_rows(
            (left_strips, left_edges, right_strips, right_edges, strip_high, edge_high, strip_low, edge_low)
        )
        row_index = jnp.arange(pieces[0].shape[0], dtype=jnp.int32)
        fine_l, edge_l = pick_from(row_index, pieces[0], pieces[1], targets_left)
        fine_r, edge_r = pick_from(row_index, pieces[2], pieces[3], targets_right)
        fine_lo, edge_lo = pick_from(row_index, pieces[4], pieces[5], targets_low)
        fine_hi, edge_hi = pick_from(row_index, pieces[6], pieces[7], targets_high)
        parts = (fine_l, edge_l, fine_r, edge_r, fine_lo, edge_lo, fine_hi, edge_hi)
        picked = tuple((extra for extra in parts))
        ghost_left = picked[0] + inject_side(picked[1])
        ghost_right = picked[2] + inject_side(picked[3])
        ghost_low = picked[4] + inject_end(picked[5])
        ghost_high = picked[6] + inject_end(picked[7])
        return jax.vmap(fine_section)(field, ghost_left, ghost_right, ghost_low, ghost_high)

    rate_f1, left_one, right_one, low_one, high_one = fine_rates(fine_box, coarse_state)
    fine_one = fine_box + rate_f1
    rate_f2, left_two, right_two, low_two, high_two = fine_rates(fine_one, coarse_one)
    fine_final = 0.5 * (fine_box + fine_one + rate_f2)
    reg_left = pair_mean(0.5 * (left_one + left_two))
    reg_right = pair_mean(0.5 * (right_one + right_two))
    reg_low = pair_mean(0.5 * (low_one + low_two))
    reg_high = pair_mean(0.5 * (high_one + high_two))
    restricted = restrict(fine_final)
    side_regs = extended(jnp.stack([reg_left, reg_right])[None], (("gx", 0),), 1)
    left_regs = side_regs[0, 1]
    right_regs = side_regs[2, 0]
    own_grid = own_table.reshape(count_y, slot_count)
    left_grid = left_table.reshape(count_y, slot_count)
    right_grid = right_table.reshape(count_y, slot_count)
    pieces = gather_rows((restricted, reg_high, reg_low, left_regs, right_regs))

    def select(hit_mask, payload):
        extra = (1,) * (payload.ndim - 2)
        return jnp.sum(
            jnp.where(hit_mask.reshape(hit_mask.shape + extra), payload, 0.0), axis=(0, 1)
        )

    parts = (
        select(own_grid == device_row, pieces[0]),
        select(own_grid == below_block, pieces[1]),
        select(own_grid == above_block, pieces[2]),
        select(left_grid == device_row, pieces[3]),
        select(right_grid == device_row, pieces[4]),
    )
    home_mean, got_below, got_above, got_left, got_right = tuple(
        (extra_part for extra_part in parts)
    )
    face_left = 0.5 * (flux_x1[:, 0] + flux_x2[:, 0])
    face_right = 0.5 * (flux_x1[:, -1] + flux_x2[:, -1])
    face_low = 0.5 * (flux_y1[:, :, 0] + flux_y2[:, :, 0])
    face_high = 0.5 * (flux_y1[:, :, -1] + flux_y2[:, :, -1])
    corr_left = jnp.where(
        refined[column_left, device_row], LAM_COARSE * (got_left - face_left), 0.0
    )
    corr_right = jnp.where(
        refined[column_right, device_row], LAM_COARSE * (face_right - got_right), 0.0
    )
    corr_low = jnp.where(refined[column, below_block], LAM_COARSE * (got_below - face_low), 0.0)
    corr_high = jnp.where(refined[column, above_block], LAM_COARSE * (face_high - got_above), 0.0)
    corr_x = jnp.concatenate(
        [
            corr_left[:, None, :],
            jnp.zeros((3, span_x - 2, span_y), jnp.float32),
            corr_right[:, None, :],
        ],
        axis=1,
    )
    corr_y = jnp.concatenate(
        [
            corr_low[:, :, None],
            jnp.zeros((3, span_x, span_y - 2), jnp.float32),
            corr_high[:, :, None],
        ],
        axis=2,
    )
    coarse_next = coarse_heun + corr_x + corr_y
    coarse_next = jnp.where(refined[column, device_row], home_mean, coarse_next)
    fine_next = jnp.where(is_live[:, None, None, None], fine_final, 0.0)[None]
    return (coarse_next, fine_next)


def solution(mesh):
    in_specs = (P(None, "gx", "gy"), P("gx", "gy", None, None, None), P())
    out_specs = (P(None, "gx", "gy"), P("gx", "gy", None, None, None))
    return jax.shard_map(shards, mesh=mesh, in_specs=in_specs, out_specs=out_specs, check_vma=False)
```

```python
import jax
import jax.numpy as jnp
from jax import lax
from jax.sharding import PartitionSpec as P

LAM_COARSE = 0.2
LAM_FINE = 0.4


def extended(cells, sides, width):
    for axis, dim in sides:
        count = lax.axis_size(axis)
        head = lax.slice_in_dim(cells, 0, width, axis=dim)
        tail = lax.slice_in_dim(cells, cells.shape[dim] - width, cells.shape[dim], axis=dim)
        cells = jnp.concatenate(
            [
                lax.ppermute(tail, axis, [(i, (i + 1) % count) for i in range(count)]),
                cells,
                lax.ppermute(head, axis, [((i + 1) % count, i) for i in range(count)]),
            ],
            axis=dim,
        )
    return cells


def face_flux_x(padded, span_x, span_y):
    cell_minus = padded[:, 0 : span_x + 1, 2 : span_y + 2]
    cell_left = padded[:, 1 : span_x + 2, 2 : span_y + 2]
    cell_right = padded[:, 2 : span_x + 3, 2 : span_y + 2]
    cell_plus = padded[:, 3 : span_x + 4, 2 : span_y + 2]
    face_mean = (7.0 * (cell_left + cell_right) - (cell_minus + cell_plus)) / 12.0
    face_jump = cell_right - cell_left
    return jnp.stack(
        [face_mean[1] - 0.5 * face_jump[0], face_mean[0] - 0.5 * face_jump[1], -0.5 * face_jump[2]]
    )


def face_flux_y(padded, span_x, span_y):
    cell_minus = padded[:, 2 : span_x + 2, 0 : span_y + 1]
    cell_left = padded[:, 2 : span_x + 2, 1 : span_y + 2]
    cell_right = padded[:, 2 : span_x + 2, 2 : span_y + 3]
    cell_plus = padded[:, 2 : span_x + 2, 3 : span_y + 4]
    face_mean = (7.0 * (cell_left + cell_right) - (cell_minus + cell_plus)) / 12.0
    face_jump = cell_right - cell_left
    return jnp.stack(
        [face_mean[2] - 0.5 * face_jump[0], -0.5 * face_jump[1], face_mean[0] - 0.5 * face_jump[2]]
    )


def advance_rate(padded, factor):
    span_x = padded.shape[1] - 4
    span_y = padded.shape[2] - 4
    flux_x = face_flux_x(padded, span_x, span_y)
    flux_y = face_flux_y(padded, span_x, span_y)
    change = -factor * (flux_x[:, 1:] - flux_x[:, :-1] + (flux_y[:, :, 1:] - flux_y[:, :, :-1]))
    return (change, flux_x, flux_y)


def inject_side(coarse_edge):
    doubled = jnp.repeat(coarse_edge, 2, axis=-1)
    return jnp.broadcast_to(doubled[..., None, :], doubled.shape[:-1] + (2, doubled.shape[-1]))


def inject_end(coarse_edge):
    doubled = jnp.repeat(coarse_edge, 2, axis=-1)
    return jnp.broadcast_to(doubled[..., None], doubled.shape + (2,))


def assemble(field, ghost_left, ghost_right, ghost_low, ghost_high):
    middle = jnp.concatenate([ghost_low, field, ghost_high], axis=-1)
    zero_band = jnp.zeros(ghost_left.shape[:-1] + (2,), field.dtype)
    left_full = jnp.concatenate([zero_band, ghost_left, zero_band], axis=-1)
    right_full = jnp.concatenate([zero_band, ghost_right, zero_band], axis=-1)
    return jnp.concatenate([left_full, middle, right_full], axis=-2)


def fine_section(field, ghost_left, ghost_right, ghost_low, ghost_high):
    padded = assemble(field, ghost_left, ghost_right, ghost_low, ghost_high)
    change, flux_x, flux_y = advance_rate(padded, LAM_FINE)
    return (change, flux_x[:, 0], flux_x[:, -1], flux_y[:, :, 0], flux_y[:, :, -1])


def pair_mean(values):
    return 0.5 * (values[..., 0::2] + values[..., 1::2])


def restrict(field):
    return 0.25 * (
        field[..., 0::2, 0::2]
        + field[..., 1::2, 0::2]
        + (field[..., 0::2, 1::2] + field[..., 1::2, 1::2])
    )


def coarse_margin(field):
    return extended(field, (("gx", 1), ("gy", 2)), 2)


def pick_from(row_index, strips, coarse_edges, targets):
    flag, fine_row, fine_sub, edge_row = targets
    sub_index = jnp.arange(strips.shape[1], dtype=jnp.int32)
    hit_mask = (
        (row_index[None, :, None] == fine_row[:, None, None])
        & (sub_index[None, None, :] == fine_sub[:, None, None])
        & flag[:, None, None]
    )
    fine_part = jnp.sum(
        jnp.where(hit_mask[:, :, :, None, None, None], strips[None], 0.0), axis=(1, 2)
    )
    edge_mask = (row_index[None, :] == edge_row[:, None]) & jnp.logical_not(flag)[:, None]
    edge_part = jnp.sum(jnp.where(edge_mask[:, :, None, None], coarse_edges[None], 0.0), axis=1)
    return (fine_part, edge_part)


def gather_rows(parts):
    flat = jnp.concatenate([part.reshape(-1) for part in parts])
    flat = jnp.pad(flat, (0, -flat.size % 1024))[None]
    rows = lax.all_gather(flat, "gy", axis=0, tiled=True)
    count = rows.shape[0]
    out = []
    offset = 0
    for part in parts:
        out.append(rows[:, offset : offset + part.size].reshape((count,) + part.shape))
        offset += part.size
    return tuple(out)


def shards(coarse_state, refined_box_state, box_parent):
    count_x = lax.axis_size("gx")
    count_y = lax.axis_size("gy")
    column = lax.axis_index("gx")
    device_row = lax.axis_index("gy")
    slot_count = refined_box_state.shape[1]
    fine_box = refined_box_state[0]
    span_x = coarse_state.shape[1]
    span_y = coarse_state.shape[2]
    block_ids = jnp.arange(count_y, dtype=jnp.int32)
    block_hits = box_parent[:, :, None] == block_ids[None, None, :]
    refined = jnp.any(block_hits, axis=1)
    slot_ids = jnp.arange(box_parent.shape[1], dtype=jnp.int32)
    slot_of = jnp.sum(jnp.where(block_hits, slot_ids[None, :, None], 0), axis=1)
    column_left = (column - 1) % count_x
    column_right = (column + 1) % count_x
    below_block = (device_row - 1) % count_y
    above_block = (device_row + 1) % count_y
    own_table = lax.dynamic_index_in_dim(box_parent, column, 0, keepdims=False)
    left_table = lax.dynamic_index_in_dim(box_parent, column_left, 0, keepdims=False)
    right_table = lax.dynamic_index_in_dim(box_parent, column_right, 0, keepdims=False)
    own_parents = lax.dynamic_slice_in_dim(own_table, device_row * slot_count, slot_count)
    is_live = own_parents < count_y
    parent = jnp.minimum(own_parents, count_y - 1)

    def fine_source(table_column, block):
        flag = refined[table_column, block]
        slot_index = slot_of[table_column, block]
        return (flag, slot_index // slot_count, slot_index % slot_count, block)

    targets_left = fine_source(column_left, parent)
    targets_right = fine_source(column_right, parent)
    targets_low = fine_source(column, (parent - 1) % count_y)
    targets_high = fine_source(column, (parent + 1) % count_y)
    rate_one, flux_x1, flux_y1 = advance_rate(coarse_margin(coarse_state), LAM_COARSE)
    coarse_one = coarse_state + rate_one
    rate_two, flux_x2, flux_y2 = advance_rate(coarse_margin(coarse_one), LAM_COARSE)
    coarse_heun = 0.5 * (coarse_state + coarse_one + rate_two)

    def fine_rates(field, coarse_now):
        strip_left = field[:, :, :2, :]
        strip_right = field[:, :, -2:, :]
        strip_low = field[..., :2]
        strip_high = field[..., -2:]
        edge_left = coarse_now[:, 0, :]
        edge_right = coarse_now[:, -1, :]
        edge_low = coarse_now[:, :, 0]
        edge_high = coarse_now[:, :, -1]
        strip_size = strip_left.size
        edge_size = edge_left.size
        side_pack = jnp.concatenate(
            [
                strip_right.reshape(-1),
                edge_right.reshape(-1),
                strip_left.reshape(-1),
                edge_left.reshape(-1),
            ]
        )[None]
        sides = extended(side_pack, (("gx", 0),), 1)
        from_left = sides[0]
        from_right = sides[2]
        left_strips = from_left[:strip_size].reshape(strip_right.shape)
        left_edges = from_left[strip_size : strip_size + edge_size].reshape(edge_right.shape)
        right_strips = from_right[strip_size + edge_size : 2 * strip_size + edge_size].reshape(
            strip_left.shape
        )
        right_edges = from_right[2 * strip_size + edge_size :].reshape(edge_left.shape)
        pieces = gather_rows(
            (left_strips, left_edges, right_strips, right_edges, strip_high, edge_high, strip_low, edge_low)
        )
        row_index = jnp.arange(pieces[0].shape[0], dtype=jnp.int32)
        fine_l, edge_l = pick_from(row_index, pieces[0], pieces[1], targets_left)
        fine_r, edge_r = pick_from(row_index, pieces[2], pieces[3], targets_right)
        fine_lo, edge_lo = pick_from(row_index, pieces[4], pieces[5], targets_low)
        fine_hi, edge_hi = pick_from(row_index, pieces[6], pieces[7], targets_high)
        parts = (fine_l, edge_l, fine_r, edge_r, fine_lo, edge_lo, fine_hi, edge_hi)
        picked = tuple((extra for extra in parts))
        ghost_left = picked[0] + inject_side(picked[1])
        ghost_right = picked[2] + inject_side(picked[3])
        ghost_low = picked[4] + inject_end(picked[5])
        ghost_high = picked[6] + inject_end(picked[7])
        return jax.vmap(fine_section)(field, ghost_left, ghost_right, ghost_low, ghost_high)

    rate_f1, left_one, right_one, low_one, high_one = fine_rates(fine_box, coarse_state)
    fine_one = fine_box + rate_f1
    rate_f2, left_two, right_two, low_two, high_two = fine_rates(fine_one, coarse_one)
    fine_final = 0.5 * (fine_box + fine_one + rate_f2)
    reg_left = pair_mean(0.5 * (left_one + left_two))
    reg_right = pair_mean(0.5 * (right_one + right_two))
    reg_low = pair_mean(0.5 * (low_one + low_two))
    reg_high = pair_mean(0.5 * (high_one + high_two))
    restricted = restrict(fine_final)
    side_regs = extended(jnp.stack([reg_left, reg_right])[None], (("gx", 0),), 1)
    left_regs = side_regs[0, 1]
    right_regs = side_regs[2, 0]
    own_grid = own_table.reshape(count_y, slot_count)
    left_grid = left_table.reshape(count_y, slot_count)
    right_grid = right_table.reshape(count_y, slot_count)
    pieces = gather_rows((restricted, reg_high, reg_low, left_regs, right_regs))

    def select(hit_mask, payload):
        extra = (1,) * (payload.ndim - 2)
        return jnp.sum(
            jnp.where(hit_mask.reshape(hit_mask.shape + extra), payload, 0.0), axis=(0, 1)
        )

    parts = (
        select(own_grid == device_row, pieces[0]),
        select(own_grid == below_block, pieces[1]),
        select(own_grid == above_block, pieces[2]),
        select(left_grid == device_row, pieces[3]),
        select(right_grid == device_row, pieces[4]),
    )
    home_mean, got_below, got_above, got_left, got_right = tuple(
        (extra_part for extra_part in parts)
    )
    face_left = 0.5 * (flux_x1[:, 0] + flux_x2[:, 0])
    face_right = 0.5 * (flux_x1[:, -1] + flux_x2[:, -1])
    face_low = 0.5 * (flux_y1[:, :, 0] + flux_y2[:, :, 0])
    face_high = 0.5 * (flux_y1[:, :, -1] + flux_y2[:, :, -1])
    corr_left = jnp.where(
        refined[column_left, device_row], LAM_COARSE * (got_left - face_left), 0.0
    )
    corr_right = jnp.where(
        refined[column_right, device_row], LAM_COARSE * (face_right - got_right), 0.0
    )
    corr_low = jnp.where(refined[column, below_block], LAM_COARSE * (got_below - face_low), 0.0)
    corr_high = jnp.where(refined[column, above_block], LAM_COARSE * (face_high - got_above), 0.0)
    corr_x = jnp.concatenate(
        [
            corr_left[:, None, :],
            jnp.zeros((3, span_x - 2, span_y), jnp.float32),
            corr_right[:, None, :],
        ],
        axis=1,
    )
    corr_y = jnp.concatenate(
        [
            corr_low[:, :, None],
            jnp.zeros((3, span_x, span_y - 2), jnp.float32),
            corr_high[:, :, None],
        ],
        axis=2,
    )
    coarse_next = coarse_heun + corr_x + corr_y
    coarse_next = jnp.where(refined[column, device_row], home_mean, coarse_next)
    fine_next = jnp.where(is_live[:, None, None, None], fine_final, 0.0)[None]
    return (coarse_next, fine_next)


def solution(mesh):
    in_specs = (P(None, "gx", "gy"), P("gx", "gy", None, None, None), P())
    out_specs = (P(None, "gx", "gy"), P("gx", "gy", None, None, None))
    return jax.shard_map(shards, mesh=mesh, in_specs=in_specs, out_specs=out_specs, check_vma=False)
```

```python
import jax
import jax.numpy as jnp
from jax import lax
from jax.sharding import PartitionSpec as P

LAM_COARSE = 0.2
LAM_FINE = 0.4


def extended(cells, sides, width):
    for axis, dim in sides:
        count = lax.axis_size(axis)
        head = lax.slice_in_dim(cells, 0, width, axis=dim)
        tail = lax.slice_in_dim(cells, cells.shape[dim] - width, cells.shape[dim], axis=dim)
        cells = jnp.concatenate(
            [
                lax.ppermute(tail, axis, [(i, (i + 1) % count) for i in range(count)]),
                cells,
                lax.ppermute(head, axis, [((i + 1) % count, i) for i in range(count)]),
            ],
            axis=dim,
        )
    return cells


def face_flux_x(padded, span_x, span_y):
    cell_minus = padded[:, 0 : span_x + 1, 2 : span_y + 2]
    cell_left = padded[:, 1 : span_x + 2, 2 : span_y + 2]
    cell_right = padded[:, 2 : span_x + 3, 2 : span_y + 2]
    cell_plus = padded[:, 3 : span_x + 4, 2 : span_y + 2]
    face_mean = (7.0 * (cell_left + cell_right) - (cell_minus + cell_plus)) / 12.0
    face_jump = cell_right - cell_left
    return jnp.stack(
        [face_mean[1] - 0.5 * face_jump[0], face_mean[0] - 0.5 * face_jump[1], -0.5 * face_jump[2]]
    )


def face_flux_y(padded, span_x, span_y):
    cell_minus = padded[:, 2 : span_x + 2, 0 : span_y + 1]
    cell_left = padded[:, 2 : span_x + 2, 1 : span_y + 2]
    cell_right = padded[:, 2 : span_x + 2, 2 : span_y + 3]
    cell_plus = padded[:, 2 : span_x + 2, 3 : span_y + 4]
    face_mean = (7.0 * (cell_left + cell_right) - (cell_minus + cell_plus)) / 12.0
    face_jump = cell_right - cell_left
    return jnp.stack(
        [face_mean[2] - 0.5 * face_jump[0], -0.5 * face_jump[1], face_mean[0] - 0.5 * face_jump[2]]
    )


def advance_rate(padded, factor):
    span_x = padded.shape[1] - 4
    span_y = padded.shape[2] - 4
    flux_x = face_flux_x(padded, span_x, span_y)
    flux_y = face_flux_y(padded, span_x, span_y)
    change = -factor * (flux_x[:, 1:] - flux_x[:, :-1] + (flux_y[:, :, 1:] - flux_y[:, :, :-1]))
    return (change, flux_x, flux_y)


def inject_side(coarse_edge):
    doubled = jnp.repeat(coarse_edge, 2, axis=-1)
    return jnp.broadcast_to(doubled[..., None, :], doubled.shape[:-1] + (2, doubled.shape[-1]))


def inject_end(coarse_edge):
    doubled = jnp.repeat(coarse_edge, 2, axis=-1)
    return jnp.broadcast_to(doubled[..., None], doubled.shape + (2,))


def assemble(field, ghost_left, ghost_right, ghost_low, ghost_high):
    middle = jnp.concatenate([ghost_low, field, ghost_high], axis=-1)
    zero_band = jnp.zeros(ghost_left.shape[:-1] + (2,), field.dtype)
    left_full = jnp.concatenate([zero_band, ghost_left, zero_band], axis=-1)
    right_full = jnp.concatenate([zero_band, ghost_right, zero_band], axis=-1)
    return jnp.concatenate([left_full, middle, right_full], axis=-2)


def fine_section(field, ghost_left, ghost_right, ghost_low, ghost_high):
    padded = assemble(field, ghost_left, ghost_right, ghost_low, ghost_high)
    change, flux_x, flux_y = advance_rate(padded, LAM_FINE)
    return (change, flux_x[:, 0], flux_x[:, -1], flux_y[:, :, 0], flux_y[:, :, -1])


def pair_mean(values):
    return 0.5 * (values[..., 0::2] + values[..., 1::2])


def restrict(field):
    return 0.25 * (
        field[..., 0::2, 0::2]
        + field[..., 1::2, 0::2]
        + (field[..., 0::2, 1::2] + field[..., 1::2, 1::2])
    )


def coarse_margin(field):
    return extended(field, (("gx", 1), ("gy", 2)), 2)


def pick_from(row_index, strips, coarse_edges, targets):
    flag, fine_row, fine_sub, edge_row = targets
    sub_index = jnp.arange(strips.shape[1], dtype=jnp.int32)
    hit_mask = (
        (row_index[None, :, None] == fine_row[:, None, None])
        & (sub_index[None, None, :] == fine_sub[:, None, None])
        & flag[:, None, None]
    )
    fine_part = jnp.sum(
        jnp.where(hit_mask[:, :, :, None, None, None], strips[None], 0.0), axis=(1, 2)
    )
    edge_mask = (row_index[None, :] == edge_row[:, None]) & jnp.logical_not(flag)[:, None]
    edge_part = jnp.sum(jnp.where(edge_mask[:, :, None, None], coarse_edges[None], 0.0), axis=1)
    return (fine_part, edge_part)


def gather_rows(parts):
    flat = jnp.concatenate([part.reshape(-1) for part in parts])
    flat = jnp.pad(flat, (0, -flat.size % 1024))[None]
    rows = lax.all_gather(flat, "gy", axis=0, tiled=True)
    count = rows.shape[0]
    out = []
    offset = 0
    for part in parts:
        out.append(rows[:, offset : offset + part.size].reshape((count,) + part.shape))
        offset += part.size
    return tuple(out)


def shards(coarse_state, refined_box_state, box_parent):
    count_x = lax.axis_size("gx")
    count_y = lax.axis_size("gy")
    column = lax.axis_index("gx")
    device_row = lax.axis_index("gy")
    slot_count = refined_box_state.shape[1]
    fine_box = refined_box_state[0]
    span_x = coarse_state.shape[1]
    span_y = coarse_state.shape[2]
    block_ids = jnp.arange(count_y, dtype=jnp.int32)
    block_hits = box_parent[:, :, None] == block_ids[None, None, :]
    refined = jnp.any(block_hits, axis=1)
    slot_ids = jnp.arange(box_parent.shape[1], dtype=jnp.int32)
    slot_of = jnp.sum(jnp.where(block_hits, slot_ids[None, :, None], 0), axis=1)
    column_left = (column - 1) % count_x
    column_right = (column + 1) % count_x
    below_block = (device_row - 1) % count_y
    above_block = (device_row + 1) % count_y
    own_table = lax.dynamic_index_in_dim(box_parent, column, 0, keepdims=False)
    left_table = lax.dynamic_index_in_dim(box_parent, column_left, 0, keepdims=False)
    right_table = lax.dynamic_index_in_dim(box_parent, column_right, 0, keepdims=False)
    own_parents = lax.dynamic_slice_in_dim(own_table, device_row * slot_count, slot_count)
    is_live = own_parents < count_y
    parent = jnp.minimum(own_parents, count_y - 1)

    def fine_source(table_column, block):
        flag = refined[table_column, block]
        slot_index = slot_of[table_column, block]
        return (flag, slot_index // slot_count, slot_index % slot_count, block)

    targets_left = fine_source(column_left, parent)
    targets_right = fine_source(column_right, parent)
    targets_low = fine_source(column, (parent - 1) % count_y)
    targets_high = fine_source(column, (parent + 1) % count_y)
    rate_one, flux_x1, flux_y1 = advance_rate(coarse_margin(coarse_state), LAM_COARSE)
    coarse_one = coarse_state + rate_one
    rate_two, flux_x2, flux_y2 = advance_rate(coarse_margin(coarse_one), LAM_COARSE)
    coarse_heun = 0.5 * (coarse_state + coarse_one + rate_two)

    def pick(gathered, source):
        flag, fine_row, fine_sub, _ = source
        row_index = jnp.arange(gathered.shape[0], dtype=jnp.int32)
        sub_index = jnp.arange(gathered.shape[1], dtype=jnp.int32)
        hit_mask = (
            (row_index[None, :, None] == fine_row[:, None, None])
            & (sub_index[None, None, :] == fine_sub[:, None, None])
            & flag[:, None, None]
        )
        extra = (1,) * (gathered.ndim - 2)
        return jnp.sum(jnp.where(hit_mask.reshape(hit_mask.shape + extra), gathered[None], 0.0), axis=(1, 2))

    def pick_edge(edges, source):
        flag, _, _, edge_row = source
        row_index = jnp.arange(edges.shape[0], dtype=jnp.int32)
        edge_mask = (row_index[None, :] == edge_row[:, None]) & jnp.logical_not(flag)[:, None]
        extra = (1,) * (edges.ndim - 1)
        return jnp.sum(jnp.where(edge_mask.reshape(edge_mask.shape + extra), edges[None], 0.0), axis=1)

    right_pack = jnp.concatenate(
        [fine_box[:, :, -4:, :].reshape(-1), coarse_state[:, -1, :].reshape(-1), coarse_one[:, -1, :].reshape(-1)]
    )
    left_pack = jnp.concatenate(
        [fine_box[:, :, :4, :].reshape(-1), coarse_state[:, 0, :].reshape(-1), coarse_one[:, 0, :].reshape(-1)]
    )
    from_left = lax.ppermute(right_pack, "gx", [(i, (i + 1) % count_x) for i in range(count_x)])
    from_right = lax.ppermute(left_pack, "gx", [((i + 1) % count_x, i) for i in range(count_x)])
    side_strip_shape = fine_box[:, :, :4, :].shape
    side_strip_size = fine_box[:, :, :4, :].size
    edge_x_shape = coarse_state[:, 0, :].shape
    edge_x_size = coarse_state[:, 0, :].size
    gathered = gather_rows(
        (
            from_left[:side_strip_size].reshape(side_strip_shape),
            from_left[side_strip_size : side_strip_size + edge_x_size].reshape(edge_x_shape),
            from_left[side_strip_size + edge_x_size :].reshape(edge_x_shape),
            from_right[:side_strip_size].reshape(side_strip_shape),
            from_right[side_strip_size : side_strip_size + edge_x_size].reshape(edge_x_shape),
            from_right[side_strip_size + edge_x_size :].reshape(edge_x_shape),
            fine_box[..., -4:],
            fine_box[..., :4],
            coarse_state[:, :, -1],
            coarse_state[:, :, 0],
            coarse_one[:, :, -1],
            coarse_one[:, :, 0],
        )
    )
    (
        left_strips,
        left_edges,
        left_edges_one,
        right_strips,
        right_edges,
        right_edges_one,
        high_strips,
        low_strips,
        high_edges,
        low_edges,
        high_edges_one,
        low_edges_one,
    ) = gathered
    targets_left_low = fine_source(column_left, (parent - 1) % count_y)
    targets_left_high = fine_source(column_left, (parent + 1) % count_y)
    targets_right_low = fine_source(column_right, (parent - 1) % count_y)
    targets_right_high = fine_source(column_right, (parent + 1) % count_y)

    def corner(strips, edges, source, rows, cols, edge_index):
        fine_part = pick(strips[:, :, :, rows[0] : rows[1], cols[0] : cols[1]], source)
        edge_part = pick_edge(edges[:, :, edge_index], source)
        return fine_part + edge_part[:, :, None, None]

    corner_left_low = corner(left_strips, left_edges, targets_left_low, (2, 4), (-2, None), -1)
    corner_left_high = corner(left_strips, left_edges, targets_left_high, (2, 4), (0, 2), 0)
    corner_right_low = corner(right_strips, right_edges, targets_right_low, (0, 2), (-2, None), -1)
    corner_right_high = corner(right_strips, right_edges, targets_right_high, (0, 2), (0, 2), 0)

    wide_left = pick(left_strips, targets_left)
    wide_right = pick(right_strips, targets_right)
    wide_low = pick(high_strips, targets_low)
    wide_high = pick(low_strips, targets_high)
    ghost_left = wide_left[:, :, 2:, :] + inject_side(pick_edge(left_edges, targets_left))
    ghost_right = wide_right[:, :, :2, :] + inject_side(pick_edge(right_edges, targets_right))
    ghost_low = wide_low[..., 2:] + inject_end(pick_edge(high_edges, targets_low))
    ghost_high = wide_high[..., :2] + inject_end(pick_edge(low_edges, targets_high))
    rate_f1, left_one, right_one, low_one, high_one = jax.vmap(fine_section)(
        fine_box, ghost_left, ghost_right, ghost_low, ghost_high
    )
    fine_one = fine_box + rate_f1

    def rim_rate(padded):
        return advance_rate(padded, LAM_FINE)[0]

    zero_pair = jnp.zeros(fine_box.shape[:2] + (2, 2), jnp.float32)

    def rows_of(low_end, middle, high_end):
        return jnp.concatenate([low_end, middle, high_end], axis=3)

    def cols_of(low_end, middle, high_end):
        return jnp.concatenate([low_end, middle, high_end], axis=2)

    padded_left = jnp.concatenate(
        [
            rows_of(zero_pair, wide_left[:, :, :2, :], zero_pair),
            rows_of(corner_left_low, wide_left[:, :, 2:, :], corner_left_high),
            rows_of(zero_pair, fine_box[:, :, :2, :], zero_pair),
        ],
        axis=2,
    )
    padded_right = jnp.concatenate(
        [
            rows_of(zero_pair, fine_box[:, :, -2:, :], zero_pair),
            rows_of(corner_right_low, wide_right[:, :, :2, :], corner_right_high),
            rows_of(zero_pair, wide_right[:, :, 2:, :], zero_pair),
        ],
        axis=2,
    )
    padded_low = jnp.concatenate(
        [
            cols_of(zero_pair, wide_low[..., :2], zero_pair),
            cols_of(corner_left_low, wide_low[..., 2:], corner_right_low),
            cols_of(zero_pair, fine_box[..., :2], zero_pair),
        ],
        axis=3,
    )
    padded_high = jnp.concatenate(
        [
            cols_of(zero_pair, fine_box[..., -2:], zero_pair),
            cols_of(corner_left_high, wide_high[..., :2], corner_right_high),
            cols_of(zero_pair, wide_high[..., 2:], zero_pair),
        ],
        axis=3,
    )
    rim_left = wide_left[:, :, 2:, :] + jax.vmap(rim_rate)(padded_left)
    rim_right = wide_right[:, :, :2, :] + jax.vmap(rim_rate)(padded_right)
    rim_low = wide_low[..., 2:] + jax.vmap(rim_rate)(padded_low)
    rim_high = wide_high[..., :2] + jax.vmap(rim_rate)(padded_high)

    def flagged(source, fine_part, coarse_part):
        return jnp.where(source[0].reshape((-1,) + (1,) * (fine_part.ndim - 1)), fine_part, coarse_part)

    ghost2_left = flagged(targets_left, rim_left, inject_side(pick_edge(left_edges_one, targets_left)))
    ghost2_right = flagged(targets_right, rim_right, inject_side(pick_edge(right_edges_one, targets_right)))
    ghost2_low = flagged(targets_low, rim_low, inject_end(pick_edge(high_edges_one, targets_low)))
    ghost2_high = flagged(targets_high, rim_high, inject_end(pick_edge(low_edges_one, targets_high)))
    rate_f2, left_two, right_two, low_two, high_two = jax.vmap(fine_section)(
        fine_one, ghost2_left, ghost2_right, ghost2_low, ghost2_high
    )
    fine_final = 0.5 * (fine_box + fine_one + rate_f2)
    reg_left = pair_mean(0.5 * (left_one + left_two))
    reg_right = pair_mean(0.5 * (right_one + right_two))
    reg_low = pair_mean(0.5 * (low_one + low_two))
    reg_high = pair_mean(0.5 * (high_one + high_two))
    restricted = restrict(fine_final)
    side_regs = extended(jnp.stack([reg_left, reg_right])[None], (("gx", 0),), 1)
    left_regs = side_regs[0, 1]
    right_regs = side_regs[2, 0]
    own_grid = own_table.reshape(count_y, slot_count)
    left_grid = left_table.reshape(count_y, slot_count)
    right_grid = right_table.reshape(count_y, slot_count)
    pieces = gather_rows((restricted, reg_high, reg_low, left_regs, right_regs))

    def select(hit_mask, payload):
        extra = (1,) * (payload.ndim - 2)
        return jnp.sum(
            jnp.where(hit_mask.reshape(hit_mask.shape + extra), payload, 0.0), axis=(0, 1)
        )

    parts = (
        select(own_grid == device_row, pieces[0]),
        select(own_grid == below_block, pieces[1]),
        select(own_grid == above_block, pieces[2]),
        select(left_grid == device_row, pieces[3]),
        select(right_grid == device_row, pieces[4]),
    )
    home_mean, got_below, got_above, got_left, got_right = tuple(
        (extra_part for extra_part in parts)
    )
    face_left = 0.5 * (flux_x1[:, 0] + flux_x2[:, 0])
    face_right = 0.5 * (flux_x1[:, -1] + flux_x2[:, -1])
    face_low = 0.5 * (flux_y1[:, :, 0] + flux_y2[:, :, 0])
    face_high = 0.5 * (flux_y1[:, :, -1] + flux_y2[:, :, -1])
    corr_left = jnp.where(
        refined[column_left, device_row], LAM_COARSE * (got_left - face_left), 0.0
    )
    corr_right = jnp.where(
        refined[column_right, device_row], LAM_COARSE * (face_right - got_right), 0.0
    )
    corr_low = jnp.where(refined[column, below_block], LAM_COARSE * (got_below - face_low), 0.0)
    corr_high = jnp.where(refined[column, above_block], LAM_COARSE * (face_high - got_above), 0.0)
    corr_x = jnp.concatenate(
        [
            corr_left[:, None, :],
            jnp.zeros((3, span_x - 2, span_y), jnp.float32),
            corr_right[:, None, :],
        ],
        axis=1,
    )
    corr_y = jnp.concatenate(
        [
            corr_low[:, :, None],
            jnp.zeros((3, span_x, span_y - 2), jnp.float32),
            corr_high[:, :, None],
        ],
        axis=2,
    )
    coarse_next = coarse_heun + corr_x + corr_y
    coarse_next = jnp.where(refined[column, device_row], home_mean, coarse_next)
    fine_next = jnp.where(is_live[:, None, None, None], fine_final, 0.0)[None]
    return (coarse_next, fine_next)


def solution(mesh):
    in_specs = (P(None, "gx", "gy"), P("gx", "gy", None, None, None), P())
    out_specs = (P(None, "gx", "gy"), P("gx", "gy", None, None, None))
    return jax.shard_map(shards, mesh=mesh, in_specs=in_specs, out_specs=out_specs, check_vma=False)
```

```python
import jax
import jax.numpy as jnp
from jax import lax
from jax.sharding import PartitionSpec as P

LAM_COARSE = 0.2
LAM_FINE = 0.4


def extended(cells, sides, width):
    for axis, dim in sides:
        count = lax.axis_size(axis)
        head = lax.slice_in_dim(cells, 0, width, axis=dim)
        tail = lax.slice_in_dim(cells, cells.shape[dim] - width, cells.shape[dim], axis=dim)
        cells = jnp.concatenate(
            [
                lax.ppermute(tail, axis, [(i, (i + 1) % count) for i in range(count)]),
                cells,
                lax.ppermute(head, axis, [((i + 1) % count, i) for i in range(count)]),
            ],
            axis=dim,
        )
    return cells


def face_flux_x(padded, span_x, span_y):
    cell_minus = padded[:, 0 : span_x + 1, 2 : span_y + 2]
    cell_left = padded[:, 1 : span_x + 2, 2 : span_y + 2]
    cell_right = padded[:, 2 : span_x + 3, 2 : span_y + 2]
    cell_plus = padded[:, 3 : span_x + 4, 2 : span_y + 2]
    face_mean = (7.0 * (cell_left + cell_right) - (cell_minus + cell_plus)) / 12.0
    face_jump = cell_right - cell_left
    return jnp.stack(
        [face_mean[1] - 0.5 * face_jump[0], face_mean[0] - 0.5 * face_jump[1], -0.5 * face_jump[2]]
    )


def face_flux_y(padded, span_x, span_y):
    cell_minus = padded[:, 2 : span_x + 2, 0 : span_y + 1]
    cell_left = padded[:, 2 : span_x + 2, 1 : span_y + 2]
    cell_right = padded[:, 2 : span_x + 2, 2 : span_y + 3]
    cell_plus = padded[:, 2 : span_x + 2, 3 : span_y + 4]
    face_mean = (7.0 * (cell_left + cell_right) - (cell_minus + cell_plus)) / 12.0
    face_jump = cell_right - cell_left
    return jnp.stack(
        [face_mean[2] - 0.5 * face_jump[0], -0.5 * face_jump[1], face_mean[0] - 0.5 * face_jump[2]]
    )


def advance_rate(padded, factor):
    span_x = padded.shape[1] - 4
    span_y = padded.shape[2] - 4
    flux_x = face_flux_x(padded, span_x, span_y)
    flux_y = face_flux_y(padded, span_x, span_y)
    change = -factor * (flux_x[:, 1:] - flux_x[:, :-1] + (flux_y[:, :, 1:] - flux_y[:, :, :-1]))
    return (change, flux_x, flux_y)


def inject_side(coarse_edge):
    doubled = jnp.repeat(coarse_edge, 2, axis=-1)
    return jnp.broadcast_to(doubled[..., None, :], doubled.shape[:-1] + (2, doubled.shape[-1]))


def inject_end(coarse_edge):
    doubled = jnp.repeat(coarse_edge, 2, axis=-1)
    return jnp.broadcast_to(doubled[..., None], doubled.shape + (2,))


def assemble(field, ghost_left, ghost_right, ghost_low, ghost_high):
    middle = jnp.concatenate([ghost_low, field, ghost_high], axis=-1)
    zero_band = jnp.zeros(ghost_left.shape[:-1] + (2,), field.dtype)
    left_full = jnp.concatenate([zero_band, ghost_left, zero_band], axis=-1)
    right_full = jnp.concatenate([zero_band, ghost_right, zero_band], axis=-1)
    return jnp.concatenate([left_full, middle, right_full], axis=-2)


def fine_section(field, ghost_left, ghost_right, ghost_low, ghost_high):
    padded = assemble(field, ghost_left, ghost_right, ghost_low, ghost_high)
    change, flux_x, flux_y = advance_rate(padded, LAM_FINE)
    return (change, flux_x[:, 0], flux_x[:, -1], flux_y[:, :, 0], flux_y[:, :, -1])


def pair_mean(values):
    return 0.5 * (values[..., 0::2] + values[..., 1::2])


def restrict(field):
    return 0.25 * (
        field[..., 0::2, 0::2]
        + field[..., 1::2, 0::2]
        + (field[..., 0::2, 1::2] + field[..., 1::2, 1::2])
    )


def coarse_margin(field):
    return extended(field, (("gx", 1), ("gy", 2)), 2)


def pick_from(row_index, strips, coarse_edges, targets):
    flag, fine_row, fine_sub, edge_row = targets
    sub_index = jnp.arange(strips.shape[1], dtype=jnp.int32)
    hit_mask = (
        (row_index[None, :, None] == fine_row[:, None, None])
        & (sub_index[None, None, :] == fine_sub[:, None, None])
        & flag[:, None, None]
    )
    fine_part = jnp.sum(
        jnp.where(hit_mask[:, :, :, None, None, None], strips[None], 0.0), axis=(1, 2)
    )
    edge_mask = (row_index[None, :] == edge_row[:, None]) & jnp.logical_not(flag)[:, None]
    edge_part = jnp.sum(jnp.where(edge_mask[:, :, None, None], coarse_edges[None], 0.0), axis=1)
    return (fine_part, edge_part)


def gather_rows(parts):
    flat = jnp.concatenate([part.reshape(-1) for part in parts])
    flat = jnp.pad(flat, (0, -flat.size % 1024))[None]
    rows = lax.all_gather(flat, "gy", axis=0, tiled=True)
    offsets = []
    offset = 0
    for part in parts:
        offsets.append((offset, part.shape))
        offset += part.size
    return rows, offsets


def take_row(rows, place, row):
    offset, shape = place
    size = 1
    for extent in shape:
        size *= extent
    return lax.dynamic_slice(rows, (row, offset), (1, size)).reshape(shape)


def take_slot(rows, place, row, sub):
    offset, shape = place
    size = 1
    for extent in shape[1:]:
        size *= extent
    return lax.dynamic_slice(rows, (row, offset + sub * size), (1, size)).reshape(shape[1:])


def shift_x(values, step):
    count = lax.axis_size("gx")
    return lax.ppermute(values, "gx", [(i, (i + step) % count) for i in range(count)])


def shift_y(values, step):
    count = lax.axis_size("gy")
    return lax.ppermute(values, "gy", [(i, (i + step) % count) for i in range(count)])


def shards(coarse_state, refined_box_state, box_parent):
    count_x = lax.axis_size("gx")
    count_y = lax.axis_size("gy")
    column = lax.axis_index("gx")
    device_row = lax.axis_index("gy")
    slot_count = refined_box_state.shape[1]
    fine_box = refined_box_state[0]
    span_x = coarse_state.shape[1]
    span_y = coarse_state.shape[2]
    block_ids = jnp.arange(count_y, dtype=jnp.int32)
    block_hits = box_parent[:, :, None] == block_ids[None, None, :]
    refined = jnp.any(block_hits, axis=1)
    slot_ids = jnp.arange(box_parent.shape[1], dtype=jnp.int32)
    slot_of = jnp.sum(jnp.where(block_hits, slot_ids[None, :, None], 0), axis=1)
    column_left = (column - 1) % count_x
    column_right = (column + 1) % count_x
    below_block = (device_row - 1) % count_y
    above_block = (device_row + 1) % count_y
    own_table = lax.dynamic_index_in_dim(box_parent, column, 0, keepdims=False)
    own_parents = lax.dynamic_slice_in_dim(own_table, device_row * slot_count, slot_count)
    is_live = own_parents < count_y
    parent = jnp.minimum(own_parents, count_y - 1)

    def fine_source(table_column, block):
        flag = refined[table_column, block]
        slot_index = slot_of[table_column, block]
        return (flag, slot_index // slot_count, slot_index % slot_count, block)

    targets_left = fine_source(column_left, parent)
    targets_right = fine_source(column_right, parent)
    targets_low = fine_source(column, (parent - 1) % count_y)
    targets_high = fine_source(column, (parent + 1) % count_y)
    targets_left_low = fine_source(column_left, (parent - 1) % count_y)
    targets_left_high = fine_source(column_left, (parent + 1) % count_y)
    targets_right_low = fine_source(column_right, (parent - 1) % count_y)
    targets_right_high = fine_source(column_right, (parent + 1) % count_y)

    strip_size = fine_box[:, :, :4, :].size
    right_pack = jnp.concatenate([fine_box[:, :, -4:, :].reshape(-1), coarse_state[:, -2:, :].reshape(-1)])
    left_pack = jnp.concatenate([fine_box[:, :, :4, :].reshape(-1), coarse_state[:, :2, :].reshape(-1)])
    from_left = shift_x(right_pack, 1)
    from_right = shift_x(left_pack, -1)
    strip_shape = fine_box[:, :, :4, :].shape
    rim_shape = coarse_state[:, :2, :].shape
    left_rim = from_left[strip_size:].reshape(rim_shape)
    right_rim = from_right[strip_size:].reshape(rim_shape)

    def coarse_padded(field, ghost_left, ghost_right):
        ghost_low = shift_y(field[:, :, -2:], 1)
        ghost_high = shift_y(field[:, :, :2], -1)
        return assemble(field, ghost_left, ghost_right, ghost_low, ghost_high)

    rate_one, flux_x1, flux_y1 = advance_rate(coarse_padded(coarse_state, left_rim, right_rim), LAM_COARSE)
    coarse_one = coarse_state + rate_one
    one_left = shift_x(coarse_one[:, -2:, :], 1)
    one_right = shift_x(coarse_one[:, :2, :], -1)
    rate_two, flux_x2, flux_y2 = advance_rate(coarse_padded(coarse_one, one_left, one_right), LAM_COARSE)
    coarse_heun = 0.5 * (coarse_state + coarse_one + rate_two)

    parts = (
        from_left[:strip_size].reshape(strip_shape),
        left_rim[:, 1, :],
        from_right[:strip_size].reshape(strip_shape),
        right_rim[:, 0, :],
        fine_box[..., -4:],
        fine_box[..., :4],
        coarse_state[:, :, -1],
        coarse_state[:, :, 0],
        coarse_one[:, :, -1],
        coarse_one[:, :, 0],
        coarse_one[:, -1, :],
        coarse_one[:, 0, :],
    )
    rows, places = gather_rows(parts)
    column_edges_one = lax.slice_in_dim(rows, places[10][0], places[10][0] + 2 * coarse_one[:, 0, :].size, axis=1)
    left_edges_one = shift_x(column_edges_one[:, : coarse_one[:, 0, :].size], 1)
    right_edges_one = shift_x(column_edges_one[:, coarse_one[:, 0, :].size :], -1)

    def pick(place, source):
        flag, fine_row, fine_sub, _ = source
        taken = jnp.stack([take_slot(rows, place, fine_row[s], fine_sub[s]) for s in range(slot_count)])
        return jnp.where(flag.reshape((-1,) + (1,) * (taken.ndim - 1)), taken, 0.0)

    def pick_edge_in(table, place, source):
        flag, _, _, edge_row = source
        taken = jnp.stack([take_row(table, place, edge_row[s]) for s in range(slot_count)])
        return jnp.where(flag.reshape((-1,) + (1,) * (taken.ndim - 1)), 0.0, taken)

    def pick_edge(place, source):
        return pick_edge_in(rows, place, source)

    def corner(place, edge_place, source, row_slice, col_slice, edge_index):
        fine_part = pick(place, source)[:, :, row_slice, col_slice]
        edge_part = pick_edge(edge_place, source)[:, :, edge_index]
        return fine_part + edge_part[:, :, None, None]

    corner_left_low = corner(places[0], places[1], targets_left_low, slice(2, 4), slice(-2, None), -1)
    corner_left_high = corner(places[0], places[1], targets_left_high, slice(2, 4), slice(0, 2), 0)
    corner_right_low = corner(places[2], places[3], targets_right_low, slice(0, 2), slice(-2, None), -1)
    corner_right_high = corner(places[2], places[3], targets_right_high, slice(0, 2), slice(0, 2), 0)

    wide_left = pick(places[0], targets_left)
    wide_right = pick(places[2], targets_right)
    wide_low = pick(places[4], targets_low)
    wide_high = pick(places[5], targets_high)
    ghost_left = wide_left[:, :, 2:, :] + inject_side(pick_edge(places[1], targets_left))
    ghost_right = wide_right[:, :, :2, :] + inject_side(pick_edge(places[3], targets_right))
    ghost_low = wide_low[..., 2:] + inject_end(pick_edge(places[6], targets_low))
    ghost_high = wide_high[..., :2] + inject_end(pick_edge(places[7], targets_high))
    rate_f1, left_one, right_one, low_one, high_one = jax.vmap(fine_section)(
        fine_box, ghost_left, ghost_right, ghost_low, ghost_high
    )
    fine_one = fine_box + rate_f1

    def rim_rate(padded):
        return advance_rate(padded, LAM_FINE)[0]

    zero_pair = jnp.zeros(fine_box.shape[:2] + (2, 2), jnp.float32)

    def rows_of(low_end, middle, high_end):
        return jnp.concatenate([low_end, middle, high_end], axis=3)

    def cols_of(low_end, middle, high_end):
        return jnp.concatenate([low_end, middle, high_end], axis=2)

    padded_left = jnp.concatenate(
        [
            rows_of(zero_pair, wide_left[:, :, :2, :], zero_pair),
            rows_of(corner_left_low, wide_left[:, :, 2:, :], corner_left_high),
            rows_of(zero_pair, fine_box[:, :, :2, :], zero_pair),
        ],
        axis=2,
    )
    padded_right = jnp.concatenate(
        [
            rows_of(zero_pair, fine_box[:, :, -2:, :], zero_pair),
            rows_of(corner_right_low, wide_right[:, :, :2, :], corner_right_high),
            rows_of(zero_pair, wide_right[:, :, 2:, :], zero_pair),
        ],
        axis=2,
    )
    padded_low = jnp.concatenate(
        [
            cols_of(zero_pair, wide_low[..., :2], zero_pair),
            cols_of(corner_left_low, wide_low[..., 2:], corner_right_low),
            cols_of(zero_pair, fine_box[..., :2], zero_pair),
        ],
        axis=3,
    )
    padded_high = jnp.concatenate(
        [
            cols_of(zero_pair, fine_box[..., -2:], zero_pair),
            cols_of(corner_left_high, wide_high[..., :2], corner_right_high),
            cols_of(zero_pair, wide_high[..., 2:], zero_pair),
        ],
        axis=3,
    )
    rim_left = wide_left[:, :, 2:, :] + jax.vmap(rim_rate)(padded_left)
    rim_right = wide_right[:, :, :2, :] + jax.vmap(rim_rate)(padded_right)
    rim_low = wide_low[..., 2:] + jax.vmap(rim_rate)(padded_low)
    rim_high = wide_high[..., :2] + jax.vmap(rim_rate)(padded_high)

    def flagged(source, fine_part, coarse_part):
        return jnp.where(source[0].reshape((-1,) + (1,) * (fine_part.ndim - 1)), fine_part, coarse_part)

    ghost2_left = flagged(targets_left, rim_left, inject_side(pick_edge_in(left_edges_one, (0, coarse_one[:, 0, :].shape), targets_left)))
    ghost2_right = flagged(targets_right, rim_right, inject_side(pick_edge_in(right_edges_one, (0, coarse_one[:, 0, :].shape), targets_right)))
    ghost2_low = flagged(targets_low, rim_low, inject_end(pick_edge(places[8], targets_low)))
    ghost2_high = flagged(targets_high, rim_high, inject_end(pick_edge(places[9], targets_high)))
    rate_f2, left_two, right_two, low_two, high_two = jax.vmap(fine_section)(
        fine_one, ghost2_left, ghost2_right, ghost2_low, ghost2_high
    )
    fine_final = 0.5 * (fine_box + fine_one + rate_f2)
    reg_left = pair_mean(0.5 * (left_one + left_two))
    reg_right = pair_mean(0.5 * (right_one + right_two))
    reg_low = pair_mean(0.5 * (low_one + low_two))
    reg_high = pair_mean(0.5 * (high_one + high_two))
    restricted = restrict(fine_final)
    left_regs = shift_x(reg_right, 1)
    right_regs = shift_x(reg_left, -1)
    rows, places = gather_rows((restricted, reg_high, reg_low, left_regs, right_regs))

    def home_pick(place, table_column, block):
        slot_index = slot_of[table_column, block]
        return take_slot(rows, place, slot_index // slot_count, slot_index % slot_count)

    home_mean = home_pick(places[0], column, device_row)
    got_below = home_pick(places[1], column, below_block)
    got_above = home_pick(places[2], column, above_block)
    got_left = home_pick(places[3], column_left, device_row)
    got_right = home_pick(places[4], column_right, device_row)
    face_left = 0.5 * (flux_x1[:, 0] + flux_x2[:, 0])
    face_right = 0.5 * (flux_x1[:, -1] + flux_x2[:, -1])
    face_low = 0.5 * (flux_y1[:, :, 0] + flux_y2[:, :, 0])
    face_high = 0.5 * (flux_y1[:, :, -1] + flux_y2[:, :, -1])
    corr_left = jnp.where(
        refined[column_left, device_row], LAM_COARSE * (got_left - face_left), 0.0
    )
    corr_right = jnp.where(
        refined[column_right, device_row], LAM_COARSE * (face_right - got_right), 0.0
    )
    corr_low = jnp.where(refined[column, below_block], LAM_COARSE * (got_below - face_low), 0.0)
    corr_high = jnp.where(refined[column, above_block], LAM_COARSE * (face_high - got_above), 0.0)
    corr_x = jnp.concatenate(
        [
            corr_left[:, None, :],
            jnp.zeros((3, span_x - 2, span_y), jnp.float32),
            corr_right[:, None, :],
        ],
        axis=1,
    )
    corr_y = jnp.concatenate(
        [
            corr_low[:, :, None],
            jnp.zeros((3, span_x, span_y - 2), jnp.float32),
            corr_high[:, :, None],
        ],
        axis=2,
    )
    coarse_next = coarse_heun + corr_x + corr_y
    coarse_next = jnp.where(refined[column, device_row], home_mean, coarse_next)
    fine_next = jnp.where(is_live[:, None, None, None], fine_final, 0.0)[None]
    return (coarse_next, fine_next)


def solution(mesh):
    in_specs = (P(None, "gx", "gy"), P("gx", "gy", None, None, None), P())
    out_specs = (P(None, "gx", "gy"), P("gx", "gy", None, None, None))
    return jax.shard_map(shards, mesh=mesh, in_specs=in_specs, out_specs=out_specs, check_vma=False)
```

```python
import jax
import jax.numpy as jnp
from jax import lax
from jax.sharding import PartitionSpec as P

LAM_COARSE = 0.2
LAM_FINE = 0.4


def extended(cells, sides, width):
    for axis, dim in sides:
        count = lax.axis_size(axis)
        head = lax.slice_in_dim(cells, 0, width, axis=dim)
        tail = lax.slice_in_dim(cells, cells.shape[dim] - width, cells.shape[dim], axis=dim)
        cells = jnp.concatenate(
            [
                lax.ppermute(tail, axis, [(i, (i + 1) % count) for i in range(count)]),
                cells,
                lax.ppermute(head, axis, [((i + 1) % count, i) for i in range(count)]),
            ],
            axis=dim,
        )
    return cells


def face_flux_x(padded, span_x, span_y):
    cell_minus = padded[:, 0 : span_x + 1, 2 : span_y + 2]
    cell_left = padded[:, 1 : span_x + 2, 2 : span_y + 2]
    cell_right = padded[:, 2 : span_x + 3, 2 : span_y + 2]
    cell_plus = padded[:, 3 : span_x + 4, 2 : span_y + 2]
    face_mean = (7.0 * (cell_left + cell_right) - (cell_minus + cell_plus)) / 12.0
    face_jump = cell_right - cell_left
    return jnp.stack(
        [face_mean[1] - 0.5 * face_jump[0], face_mean[0] - 0.5 * face_jump[1], -0.5 * face_jump[2]]
    )


def face_flux_y(padded, span_x, span_y):
    cell_minus = padded[:, 2 : span_x + 2, 0 : span_y + 1]
    cell_left = padded[:, 2 : span_x + 2, 1 : span_y + 2]
    cell_right = padded[:, 2 : span_x + 2, 2 : span_y + 3]
    cell_plus = padded[:, 2 : span_x + 2, 3 : span_y + 4]
    face_mean = (7.0 * (cell_left + cell_right) - (cell_minus + cell_plus)) / 12.0
    face_jump = cell_right - cell_left
    return jnp.stack(
        [face_mean[2] - 0.5 * face_jump[0], -0.5 * face_jump[1], face_mean[0] - 0.5 * face_jump[2]]
    )


def advance_rate(padded, factor):
    span_x = padded.shape[1] - 4
    span_y = padded.shape[2] - 4
    flux_x = face_flux_x(padded, span_x, span_y)
    flux_y = face_flux_y(padded, span_x, span_y)
    change = -factor * (flux_x[:, 1:] - flux_x[:, :-1] + (flux_y[:, :, 1:] - flux_y[:, :, :-1]))
    return (change, flux_x, flux_y)


def inject_side(coarse_edge):
    doubled = jnp.repeat(coarse_edge, 2, axis=-1)
    return jnp.broadcast_to(doubled[..., None, :], doubled.shape[:-1] + (2, doubled.shape[-1]))


def inject_end(coarse_edge):
    doubled = jnp.repeat(coarse_edge, 2, axis=-1)
    return jnp.broadcast_to(doubled[..., None], doubled.shape + (2,))


def assemble(field, ghost_left, ghost_right, ghost_low, ghost_high):
    middle = jnp.concatenate([ghost_low, field, ghost_high], axis=-1)
    zero_band = jnp.zeros(ghost_left.shape[:-1] + (2,), field.dtype)
    left_full = jnp.concatenate([zero_band, ghost_left, zero_band], axis=-1)
    right_full = jnp.concatenate([zero_band, ghost_right, zero_band], axis=-1)
    return jnp.concatenate([left_full, middle, right_full], axis=-2)


def fine_section(field, ghost_left, ghost_right, ghost_low, ghost_high):
    padded = assemble(field, ghost_left, ghost_right, ghost_low, ghost_high)
    change, flux_x, flux_y = advance_rate(padded, LAM_FINE)
    return (change, flux_x[:, 0], flux_x[:, -1], flux_y[:, :, 0], flux_y[:, :, -1])


def pair_mean(values):
    return 0.5 * (values[..., 0::2] + values[..., 1::2])


def restrict(field):
    return 0.25 * (
        field[..., 0::2, 0::2]
        + field[..., 1::2, 0::2]
        + (field[..., 0::2, 1::2] + field[..., 1::2, 1::2])
    )


def coarse_margin(field):
    return extended(field, (("gx", 1), ("gy", 2)), 2)


def pick_from(row_index, strips, coarse_edges, targets):
    flag, fine_row, fine_sub, edge_row = targets
    sub_index = jnp.arange(strips.shape[1], dtype=jnp.int32)
    hit_mask = (
        (row_index[None, :, None] == fine_row[:, None, None])
        & (sub_index[None, None, :] == fine_sub[:, None, None])
        & flag[:, None, None]
    )
    fine_part = jnp.sum(
        jnp.where(hit_mask[:, :, :, None, None, None], strips[None], 0.0), axis=(1, 2)
    )
    edge_mask = (row_index[None, :] == edge_row[:, None]) & jnp.logical_not(flag)[:, None]
    edge_part = jnp.sum(jnp.where(edge_mask[:, :, None, None], coarse_edges[None], 0.0), axis=1)
    return (fine_part, edge_part)


def gather_rows(parts):
    flat = jnp.concatenate([part.reshape(-1) for part in parts])
    flat = jnp.pad(flat, (0, -flat.size % 1024))[None]
    rows = lax.all_gather(flat, "gy", axis=0, tiled=True)
    offsets = []
    offset = 0
    for part in parts:
        offsets.append((offset, part.shape))
        offset += part.size
    return rows, offsets


def take_row(rows, place, row):
    offset, shape = place
    size = 1
    for extent in shape:
        size *= extent
    return lax.dynamic_slice(rows, (row, offset), (1, size)).reshape(shape)


def take_slot(rows, place, row, sub):
    offset, shape = place
    size = 1
    for extent in shape[1:]:
        size *= extent
    return lax.dynamic_slice(rows, (row, offset + sub * size), (1, size)).reshape(shape[1:])


def shift_x(values, step):
    count = lax.axis_size("gx")
    return lax.ppermute(values, "gx", [(i, (i + step) % count) for i in range(count)])


def shift_y(values, step):
    count = lax.axis_size("gy")
    return lax.ppermute(values, "gy", [(i, (i + step) % count) for i in range(count)])


def shards(coarse_state, refined_box_state, box_parent):
    count_x = lax.axis_size("gx")
    count_y = lax.axis_size("gy")
    column = lax.axis_index("gx")
    device_row = lax.axis_index("gy")
    slot_count = refined_box_state.shape[1]
    fine_box = refined_box_state[0]
    span_x = coarse_state.shape[1]
    span_y = coarse_state.shape[2]
    block_ids = jnp.arange(count_y, dtype=jnp.int32)
    block_hits = box_parent[:, :, None] == block_ids[None, None, :]
    refined = jnp.any(block_hits, axis=1)
    slot_ids = jnp.arange(box_parent.shape[1], dtype=jnp.int32)
    slot_of = jnp.sum(jnp.where(block_hits, slot_ids[None, :, None], 0), axis=1)
    column_left = (column - 1) % count_x
    column_right = (column + 1) % count_x
    below_block = (device_row - 1) % count_y
    above_block = (device_row + 1) % count_y
    own_table = lax.dynamic_index_in_dim(box_parent, column, 0, keepdims=False)
    own_parents = lax.dynamic_slice_in_dim(own_table, device_row * slot_count, slot_count)
    is_live = own_parents < count_y
    parent = jnp.minimum(own_parents, count_y - 1)

    def fine_source(table_column, block):
        flag = refined[table_column, block]
        slot_index = slot_of[table_column, block]
        return (flag, slot_index // slot_count, slot_index % slot_count, block)

    targets_left = fine_source(column_left, parent)
    targets_right = fine_source(column_right, parent)
    targets_low = fine_source(column, (parent - 1) % count_y)
    targets_high = fine_source(column, (parent + 1) % count_y)
    targets_left_low = fine_source(column_left, (parent - 1) % count_y)
    targets_left_high = fine_source(column_left, (parent + 1) % count_y)
    targets_right_low = fine_source(column_right, (parent - 1) % count_y)
    targets_right_high = fine_source(column_right, (parent + 1) % count_y)

    strip_size = fine_box[:, :, :4, :].size
    right_pack = jnp.concatenate([fine_box[:, :, -4:, :].reshape(-1), coarse_state[:, -3:, :].reshape(-1)])
    left_pack = jnp.concatenate([fine_box[:, :, :4, :].reshape(-1), coarse_state[:, :3, :].reshape(-1)])
    from_left = shift_x(right_pack, 1)
    from_right = shift_x(left_pack, -1)
    strip_shape = fine_box[:, :, :4, :].shape
    rim_shape = coarse_state[:, :3, :].shape
    left_rows = from_left[strip_size:].reshape(rim_shape)
    right_rows = from_right[strip_size:].reshape(rim_shape)
    left_rim = left_rows[:, 1:, :]
    right_rim = right_rows[:, :2, :]

    def coarse_padded(field, ghost_left, ghost_right):
        ghost_low = shift_y(field[:, :, -2:], 1)
        ghost_high = shift_y(field[:, :, :2], -1)
        return assemble(field, ghost_left, ghost_right, ghost_low, ghost_high)

    rate_one, flux_x1, flux_y1 = advance_rate(coarse_padded(coarse_state, left_rim, right_rim), LAM_COARSE)
    coarse_one = coarse_state + rate_one
    one_left = shift_x(coarse_one[:, -2:, :], 1)
    one_right = shift_x(coarse_one[:, :2, :], -1)
    rate_two, flux_x2, flux_y2 = advance_rate(coarse_padded(coarse_one, one_left, one_right), LAM_COARSE)
    coarse_heun = 0.5 * (coarse_state + coarse_one + rate_two)

    parts = (
        from_left[:strip_size].reshape(strip_shape),
        left_rows,
        from_right[:strip_size].reshape(strip_shape),
        right_rows,
        fine_box[..., -4:],
        fine_box[..., :4],
        coarse_state[:, :, -1],
        coarse_state[:, :, 0],
        coarse_one[:, :, -1],
        coarse_one[:, :, 0],
        coarse_state[:, :2, :],
        coarse_state[:, -2:, :],
    )
    rows, places = gather_rows(parts)

    def pick(place, source):
        flag, fine_row, fine_sub, _ = source
        taken = jnp.stack([take_slot(rows, place, fine_row[s], fine_sub[s]) for s in range(slot_count)])
        return jnp.where(flag.reshape((-1,) + (1,) * (taken.ndim - 1)), taken, 0.0)

    def pick_edge_in(table, place, source):
        flag, _, _, edge_row = source
        taken = jnp.stack([take_row(table, place, edge_row[s]) for s in range(slot_count)])
        return jnp.where(flag.reshape((-1,) + (1,) * (taken.ndim - 1)), 0.0, taken)

    def pick_edge(place, source):
        return pick_edge_in(rows, place, source)

    def corner(place, edge_place, source, row_slice, col_slice, edge_row, edge_index):
        fine_part = pick(place, source)[:, :, row_slice, col_slice]
        edge_part = pick_edge(edge_place, source)[:, :, edge_row, edge_index]
        return fine_part + edge_part[:, :, None, None]

    corner_left_low = corner(places[0], places[1], targets_left_low, slice(2, 4), slice(-2, None), 2, -1)
    corner_left_high = corner(places[0], places[1], targets_left_high, slice(2, 4), slice(0, 2), 2, 0)
    corner_right_low = corner(places[2], places[3], targets_right_low, slice(0, 2), slice(-2, None), 0, -1)
    corner_right_high = corner(places[2], places[3], targets_right_high, slice(0, 2), slice(0, 2), 0, 0)

    wide_left = pick(places[0], targets_left)
    wide_right = pick(places[2], targets_right)
    wide_low = pick(places[4], targets_low)
    wide_high = pick(places[5], targets_high)
    ghost_left = wide_left[:, :, 2:, :] + inject_side(pick_edge(places[1], targets_left)[:, :, 2, :])
    ghost_right = wide_right[:, :, :2, :] + inject_side(pick_edge(places[3], targets_right)[:, :, 0, :])
    ghost_low = wide_low[..., 2:] + inject_end(pick_edge(places[6], targets_low))
    ghost_high = wide_high[..., :2] + inject_end(pick_edge(places[7], targets_high))
    rate_f1, left_one, right_one, low_one, high_one = jax.vmap(fine_section)(
        fine_box, ghost_left, ghost_right, ghost_low, ghost_high
    )
    fine_one = fine_box + rate_f1

    def rim_rate(padded):
        return advance_rate(padded, LAM_FINE)[0]

    zero_pair = jnp.zeros(fine_box.shape[:2] + (2, 2), jnp.float32)

    def rows_of(low_end, middle, high_end):
        return jnp.concatenate([low_end, middle, high_end], axis=3)

    def cols_of(low_end, middle, high_end):
        return jnp.concatenate([low_end, middle, high_end], axis=2)

    padded_left = jnp.concatenate(
        [
            rows_of(zero_pair, wide_left[:, :, :2, :], zero_pair),
            rows_of(corner_left_low, wide_left[:, :, 2:, :], corner_left_high),
            rows_of(zero_pair, fine_box[:, :, :2, :], zero_pair),
        ],
        axis=2,
    )
    padded_right = jnp.concatenate(
        [
            rows_of(zero_pair, fine_box[:, :, -2:, :], zero_pair),
            rows_of(corner_right_low, wide_right[:, :, :2, :], corner_right_high),
            rows_of(zero_pair, wide_right[:, :, 2:, :], zero_pair),
        ],
        axis=2,
    )
    padded_low = jnp.concatenate(
        [
            cols_of(zero_pair, wide_low[..., :2], zero_pair),
            cols_of(corner_left_low, wide_low[..., 2:], corner_right_low),
            cols_of(zero_pair, fine_box[..., :2], zero_pair),
        ],
        axis=3,
    )
    padded_high = jnp.concatenate(
        [
            cols_of(zero_pair, fine_box[..., -2:], zero_pair),
            cols_of(corner_left_high, wide_high[..., :2], corner_right_high),
            cols_of(zero_pair, wide_high[..., 2:], zero_pair),
        ],
        axis=3,
    )
    rim_left = wide_left[:, :, 2:, :] + jax.vmap(rim_rate)(padded_left)
    rim_right = wide_right[:, :, :2, :] + jax.vmap(rim_rate)(padded_right)
    rim_low = wide_low[..., 2:] + jax.vmap(rim_rate)(padded_low)
    rim_high = wide_high[..., :2] + jax.vmap(rim_rate)(padded_high)

    def side_step_one(block, far_place, far_row, near_place, far_first):
        far = take_row(rows, far_place, block)
        near = take_row(rows, near_place, block)
        below = take_row(rows, far_place, (block - 1) % count_y)[:, far_row, -2:]
        above = take_row(rows, far_place, (block + 1) % count_y)[:, far_row, :2]
        zero_band = jnp.zeros((far.shape[0], 2, 2), jnp.float32)
        line = jnp.concatenate([below[:, None, :], far[:, far_row : far_row + 1, :], above[:, None, :]], axis=2)
        if far_first:
            outer = jnp.concatenate([zero_band, far[:, :2, :], zero_band], axis=2)
            inner = jnp.concatenate([zero_band, near, zero_band], axis=2)
            padded = jnp.concatenate([outer, line, inner], axis=1)
        else:
            inner = jnp.concatenate([zero_band, near, zero_band], axis=2)
            outer = jnp.concatenate([zero_band, far[:, 1:, :], zero_band], axis=2)
            padded = jnp.concatenate([inner, line, outer], axis=1)
        return far[:, far_row, :] + advance_rate(padded, LAM_COARSE)[0][:, 0, :]

    edge_one_left = jnp.stack(
        [side_step_one(parent[s], places[1], 2, places[10], True) for s in range(slot_count)]
    )
    edge_one_right = jnp.stack(
        [side_step_one(parent[s], places[3], 0, places[11], False) for s in range(slot_count)]
    )

    def flagged(source, fine_part, coarse_part):
        return jnp.where(source[0].reshape((-1,) + (1,) * (fine_part.ndim - 1)), fine_part, coarse_part)

    ghost2_left = flagged(targets_left, rim_left, inject_side(edge_one_left))
    ghost2_right = flagged(targets_right, rim_right, inject_side(edge_one_right))
    ghost2_low = flagged(targets_low, rim_low, inject_end(pick_edge(places[8], targets_low)))
    ghost2_high = flagged(targets_high, rim_high, inject_end(pick_edge(places[9], targets_high)))
    rate_f2, left_two, right_two, low_two, high_two = jax.vmap(fine_section)(
        fine_one, ghost2_left, ghost2_right, ghost2_low, ghost2_high
    )
    fine_final = 0.5 * (fine_box + fine_one + rate_f2)
    reg_left = pair_mean(0.5 * (left_one + left_two))
    reg_right = pair_mean(0.5 * (right_one + right_two))
    reg_low = pair_mean(0.5 * (low_one + low_two))
    reg_high = pair_mean(0.5 * (high_one + high_two))
    restricted = restrict(fine_final)
    left_regs = shift_x(reg_right, 1)
    right_regs = shift_x(reg_left, -1)
    rows, places = gather_rows((restricted, reg_high, reg_low, left_regs, right_regs))

    def home_pick(place, table_column, block):
        slot_index = slot_of[table_column, block]
        return take_slot(rows, place, slot_index // slot_count, slot_index % slot_count)

    home_mean = home_pick(places[0], column, device_row)
    got_below = home_pick(places[1], column, below_block)
    got_above = home_pick(places[2], column, above_block)
    got_left = home_pick(places[3], column_left, device_row)
    got_right = home_pick(places[4], column_right, device_row)
    face_left = 0.5 * (flux_x1[:, 0] + flux_x2[:, 0])
    face_right = 0.5 * (flux_x1[:, -1] + flux_x2[:, -1])
    face_low = 0.5 * (flux_y1[:, :, 0] + flux_y2[:, :, 0])
    face_high = 0.5 * (flux_y1[:, :, -1] + flux_y2[:, :, -1])
    corr_left = jnp.where(
        refined[column_left, device_row], LAM_COARSE * (got_left - face_left), 0.0
    )
    corr_right = jnp.where(
        refined[column_right, device_row], LAM_COARSE * (face_right - got_right), 0.0
    )
    corr_low = jnp.where(refined[column, below_block], LAM_COARSE * (got_below - face_low), 0.0)
    corr_high = jnp.where(refined[column, above_block], LAM_COARSE * (face_high - got_above), 0.0)
    corr_x = jnp.concatenate(
        [
            corr_left[:, None, :],
            jnp.zeros((3, span_x - 2, span_y), jnp.float32),
            corr_right[:, None, :],
        ],
        axis=1,
    )
    corr_y = jnp.concatenate(
        [
            corr_low[:, :, None],
            jnp.zeros((3, span_x, span_y - 2), jnp.float32),
            corr_high[:, :, None],
        ],
        axis=2,
    )
    coarse_next = coarse_heun + corr_x + corr_y
    coarse_next = jnp.where(refined[column, device_row], home_mean, coarse_next)
    fine_next = jnp.where(is_live[:, None, None, None], fine_final, 0.0)[None]
    return (coarse_next, fine_next)


def solution(mesh):
    in_specs = (P(None, "gx", "gy"), P("gx", "gy", None, None, None), P())
    out_specs = (P(None, "gx", "gy"), P("gx", "gy", None, None, None))
    return jax.shard_map(shards, mesh=mesh, in_specs=in_specs, out_specs=out_specs, check_vma=False)
```

```python
import jax
import jax.numpy as jnp
from jax import lax
from jax.sharding import PartitionSpec as P

LAM_COARSE = 0.2
LAM_FINE = 0.4


def extended(cells, sides, width):
    for axis, dim in sides:
        count = lax.axis_size(axis)
        head = lax.slice_in_dim(cells, 0, width, axis=dim)
        tail = lax.slice_in_dim(cells, cells.shape[dim] - width, cells.shape[dim], axis=dim)
        cells = jnp.concatenate(
            [
                lax.ppermute(tail, axis, [(i, (i + 1) % count) for i in range(count)]),
                cells,
                lax.ppermute(head, axis, [((i + 1) % count, i) for i in range(count)]),
            ],
            axis=dim,
        )
    return cells


def face_flux_x(padded, span_x, span_y):
    cell_minus = padded[:, 0 : span_x + 1, 2 : span_y + 2]
    cell_left = padded[:, 1 : span_x + 2, 2 : span_y + 2]
    cell_right = padded[:, 2 : span_x + 3, 2 : span_y + 2]
    cell_plus = padded[:, 3 : span_x + 4, 2 : span_y + 2]
    face_mean = (7.0 * (cell_left + cell_right) - (cell_minus + cell_plus)) / 12.0
    face_jump = cell_right - cell_left
    return jnp.stack(
        [face_mean[1] - 0.5 * face_jump[0], face_mean[0] - 0.5 * face_jump[1], -0.5 * face_jump[2]]
    )


def face_flux_y(padded, span_x, span_y):
    cell_minus = padded[:, 2 : span_x + 2, 0 : span_y + 1]
    cell_left = padded[:, 2 : span_x + 2, 1 : span_y + 2]
    cell_right = padded[:, 2 : span_x + 2, 2 : span_y + 3]
    cell_plus = padded[:, 2 : span_x + 2, 3 : span_y + 4]
    face_mean = (7.0 * (cell_left + cell_right) - (cell_minus + cell_plus)) / 12.0
    face_jump = cell_right - cell_left
    return jnp.stack(
        [face_mean[2] - 0.5 * face_jump[0], -0.5 * face_jump[1], face_mean[0] - 0.5 * face_jump[2]]
    )


def advance_rate(padded, factor):
    span_x = padded.shape[1] - 4
    span_y = padded.shape[2] - 4
    flux_x = face_flux_x(padded, span_x, span_y)
    flux_y = face_flux_y(padded, span_x, span_y)
    change = -factor * (flux_x[:, 1:] - flux_x[:, :-1] + (flux_y[:, :, 1:] - flux_y[:, :, :-1]))
    return (change, flux_x, flux_y)


def inject_side(coarse_edge):
    doubled = jnp.repeat(coarse_edge, 2, axis=-1)
    return jnp.broadcast_to(doubled[..., None, :], doubled.shape[:-1] + (2, doubled.shape[-1]))


def inject_end(coarse_edge):
    doubled = jnp.repeat(coarse_edge, 2, axis=-1)
    return jnp.broadcast_to(doubled[..., None], doubled.shape + (2,))


def assemble(field, ghost_left, ghost_right, ghost_low, ghost_high):
    middle = jnp.concatenate([ghost_low, field, ghost_high], axis=-1)
    zero_band = jnp.zeros(ghost_left.shape[:-1] + (2,), field.dtype)
    left_full = jnp.concatenate([zero_band, ghost_left, zero_band], axis=-1)
    right_full = jnp.concatenate([zero_band, ghost_right, zero_band], axis=-1)
    return jnp.concatenate([left_full, middle, right_full], axis=-2)


def fine_section(field, ghost_left, ghost_right, ghost_low, ghost_high):
    padded = assemble(field, ghost_left, ghost_right, ghost_low, ghost_high)
    change, flux_x, flux_y = advance_rate(padded, LAM_FINE)
    return (change, flux_x[:, 0], flux_x[:, -1], flux_y[:, :, 0], flux_y[:, :, -1])


def pair_mean(values):
    return 0.5 * (values[..., 0::2] + values[..., 1::2])


def restrict(field):
    paired = field[..., 0::2, :] + field[..., 1::2, :]
    return 0.25 * (paired[..., 0::2] + paired[..., 1::2])


def coarse_margin(field):
    return extended(field, (("gx", 1), ("gy", 2)), 2)


def pick_from(row_index, strips, coarse_edges, targets):
    flag, fine_row, fine_sub, edge_row = targets
    sub_index = jnp.arange(strips.shape[1], dtype=jnp.int32)
    hit_mask = (
        (row_index[None, :, None] == fine_row[:, None, None])
        & (sub_index[None, None, :] == fine_sub[:, None, None])
        & flag[:, None, None]
    )
    fine_part = jnp.sum(
        jnp.where(hit_mask[:, :, :, None, None, None], strips[None], 0.0), axis=(1, 2)
    )
    edge_mask = (row_index[None, :] == edge_row[:, None]) & jnp.logical_not(flag)[:, None]
    edge_part = jnp.sum(jnp.where(edge_mask[:, :, None, None], coarse_edges[None], 0.0), axis=1)
    return (fine_part, edge_part)


def gather_rows(parts):
    flat = jnp.concatenate([part.reshape(-1) for part in parts])
    flat = jnp.pad(flat, (0, -flat.size % 1024))[None]
    rows = lax.all_gather(flat, "gy", axis=0, tiled=True)
    offsets = []
    offset = 0
    for part in parts:
        offsets.append((offset, part.shape))
        offset += part.size
    return rows, offsets


def take_row(rows, place, row):
    offset, shape = place
    size = 1
    for extent in shape:
        size *= extent
    return lax.dynamic_slice(rows, (row, offset), (1, size)).reshape(shape)


def take_slot(rows, place, row, sub):
    offset, shape = place
    size = 1
    for extent in shape[1:]:
        size *= extent
    return lax.dynamic_slice(rows, (row, offset + sub * size), (1, size)).reshape(shape[1:])


def shift_x(values, step):
    count = lax.axis_size("gx")
    return lax.ppermute(values, "gx", [(i, (i + step) % count) for i in range(count)])


def shift_y(values, step):
    count = lax.axis_size("gy")
    return lax.ppermute(values, "gy", [(i, (i + step) % count) for i in range(count)])


def shards(coarse_state, refined_box_state, box_parent):
    count_x = lax.axis_size("gx")
    count_y = lax.axis_size("gy")
    column = lax.axis_index("gx")
    device_row = lax.axis_index("gy")
    slot_count = refined_box_state.shape[1]
    fine_box = refined_box_state[0]
    span_x = coarse_state.shape[1]
    span_y = coarse_state.shape[2]
    block_ids = jnp.arange(count_y, dtype=jnp.int32)
    block_hits = box_parent[:, :, None] == block_ids[None, None, :]
    refined = jnp.any(block_hits, axis=1)
    slot_ids = jnp.arange(box_parent.shape[1], dtype=jnp.int32)
    slot_of = jnp.sum(jnp.where(block_hits, slot_ids[None, :, None], 0), axis=1)
    column_left = (column - 1) % count_x
    column_right = (column + 1) % count_x
    below_block = (device_row - 1) % count_y
    above_block = (device_row + 1) % count_y
    own_table = lax.dynamic_index_in_dim(box_parent, column, 0, keepdims=False)
    own_parents = lax.dynamic_slice_in_dim(own_table, device_row * slot_count, slot_count)
    is_live = own_parents < count_y
    parent = jnp.minimum(own_parents, count_y - 1)

    def fine_source(table_column, block):
        flag = refined[table_column, block]
        slot_index = slot_of[table_column, block]
        return (flag, slot_index // slot_count, slot_index % slot_count, block)

    targets_left = fine_source(column_left, parent)
    targets_right = fine_source(column_right, parent)
    targets_low = fine_source(column, (parent - 1) % count_y)
    targets_high = fine_source(column, (parent + 1) % count_y)
    targets_left_low = fine_source(column_left, (parent - 1) % count_y)
    targets_left_high = fine_source(column_left, (parent + 1) % count_y)
    targets_right_low = fine_source(column_right, (parent - 1) % count_y)
    targets_right_high = fine_source(column_right, (parent + 1) % count_y)

    strip_size = fine_box[:, :, :4, :].size
    right_pack = jnp.concatenate([fine_box[:, :, -4:, :].reshape(-1), coarse_state[:, -2:, :].reshape(-1)])
    left_pack = jnp.concatenate([fine_box[:, :, :4, :].reshape(-1), coarse_state[:, :2, :].reshape(-1)])
    from_left = shift_x(right_pack, 1)
    from_right = shift_x(left_pack, -1)
    strip_shape = fine_box[:, :, :4, :].shape
    rim_shape = coarse_state[:, :2, :].shape
    left_rim = from_left[strip_size:].reshape(rim_shape)
    right_rim = from_right[strip_size:].reshape(rim_shape)

    def coarse_padded(field, ghost_left, ghost_right):
        ghost_low = shift_y(field[:, :, -2:], 1)
        ghost_high = shift_y(field[:, :, :2], -1)
        return assemble(field, ghost_left, ghost_right, ghost_low, ghost_high)

    rate_one, flux_x1, flux_y1 = advance_rate(coarse_padded(coarse_state, left_rim, right_rim), LAM_COARSE)
    coarse_one = coarse_state + rate_one
    one_left = shift_x(coarse_one[:, -2:, :], 1)
    one_right = shift_x(coarse_one[:, :2, :], -1)
    rate_two, flux_x2, flux_y2 = advance_rate(coarse_padded(coarse_one, one_left, one_right), LAM_COARSE)
    coarse_heun = 0.5 * (coarse_state + coarse_one + rate_two)

    parts = (
        from_left[:strip_size].reshape(strip_shape),
        left_rim[:, 1, :],
        from_right[:strip_size].reshape(strip_shape),
        right_rim[:, 0, :],
        fine_box[..., -4:],
        fine_box[..., :4],
        coarse_state[:, :, -1],
        coarse_state[:, :, 0],
        coarse_one[:, :, -1],
        coarse_one[:, :, 0],
        coarse_one[:, -1, :],
        coarse_one[:, 0, :],
    )
    rows, places = gather_rows(parts)
    column_edges_one = lax.slice_in_dim(rows, places[10][0], places[10][0] + 2 * coarse_one[:, 0, :].size, axis=1)
    left_edges_one = shift_x(column_edges_one[:, : coarse_one[:, 0, :].size], 1)
    right_edges_one = shift_x(column_edges_one[:, coarse_one[:, 0, :].size :], -1)

    def pick(place, source):
        flag, fine_row, fine_sub, _ = source
        taken = jnp.stack([take_slot(rows, place, fine_row[s], fine_sub[s]) for s in range(slot_count)])
        return jnp.where(flag.reshape((-1,) + (1,) * (taken.ndim - 1)), taken, 0.0)

    def pick_edge_in(table, place, source):
        flag, _, _, edge_row = source
        taken = jnp.stack([take_row(table, place, edge_row[s]) for s in range(slot_count)])
        return jnp.where(flag.reshape((-1,) + (1,) * (taken.ndim - 1)), 0.0, taken)

    def pick_edge(place, source):
        return pick_edge_in(rows, place, source)

    def corner(place, edge_place, source, row_slice, col_slice, edge_index):
        fine_part = pick(place, source)[:, :, row_slice, col_slice]
        edge_part = pick_edge(edge_place, source)[:, :, edge_index]
        return fine_part + edge_part[:, :, None, None]

    corner_left_low = corner(places[0], places[1], targets_left_low, slice(2, 4), slice(-2, None), -1)
    corner_left_high = corner(places[0], places[1], targets_left_high, slice(2, 4), slice(0, 2), 0)
    corner_right_low = corner(places[2], places[3], targets_right_low, slice(0, 2), slice(-2, None), -1)
    corner_right_high = corner(places[2], places[3], targets_right_high, slice(0, 2), slice(0, 2), 0)

    wide_left = pick(places[0], targets_left)
    wide_right = pick(places[2], targets_right)
    wide_low = pick(places[4], targets_low)
    wide_high = pick(places[5], targets_high)
    ghost_left = wide_left[:, :, 2:, :] + inject_side(pick_edge(places[1], targets_left))
    ghost_right = wide_right[:, :, :2, :] + inject_side(pick_edge(places[3], targets_right))
    ghost_low = wide_low[..., 2:] + inject_end(pick_edge(places[6], targets_low))
    ghost_high = wide_high[..., :2] + inject_end(pick_edge(places[7], targets_high))
    rate_f1, left_one, right_one, low_one, high_one = jax.vmap(fine_section)(
        fine_box, ghost_left, ghost_right, ghost_low, ghost_high
    )
    fine_one = fine_box + rate_f1

    def rim_rate(padded):
        return advance_rate(padded, LAM_FINE)[0]

    zero_pair = jnp.zeros(fine_box.shape[:2] + (2, 2), jnp.float32)

    def rows_of(low_end, middle, high_end):
        return jnp.concatenate([low_end, middle, high_end], axis=3)

    def cols_of(low_end, middle, high_end):
        return jnp.concatenate([low_end, middle, high_end], axis=2)

    padded_left = jnp.concatenate(
        [
            rows_of(zero_pair, wide_left[:, :, :2, :], zero_pair),
            rows_of(corner_left_low, wide_left[:, :, 2:, :], corner_left_high),
            rows_of(zero_pair, fine_box[:, :, :2, :], zero_pair),
        ],
        axis=2,
    )
    padded_right = jnp.concatenate(
        [
            rows_of(zero_pair, fine_box[:, :, -2:, :], zero_pair),
            rows_of(corner_right_low, wide_right[:, :, :2, :], corner_right_high),
            rows_of(zero_pair, wide_right[:, :, 2:, :], zero_pair),
        ],
        axis=2,
    )
    padded_low = jnp.concatenate(
        [
            cols_of(zero_pair, wide_low[..., :2], zero_pair),
            cols_of(corner_left_low, wide_low[..., 2:], corner_right_low),
            cols_of(zero_pair, fine_box[..., :2], zero_pair),
        ],
        axis=3,
    )
    padded_high = jnp.concatenate(
        [
            cols_of(zero_pair, fine_box[..., -2:], zero_pair),
            cols_of(corner_left_high, wide_high[..., :2], corner_right_high),
            cols_of(zero_pair, wide_high[..., 2:], zero_pair),
        ],
        axis=3,
    )
    rim_left = wide_left[:, :, 2:, :] + jax.vmap(rim_rate)(padded_left)
    rim_right = wide_right[:, :, :2, :] + jax.vmap(rim_rate)(padded_right)
    rim_low = wide_low[..., 2:] + jax.vmap(rim_rate)(padded_low)
    rim_high = wide_high[..., :2] + jax.vmap(rim_rate)(padded_high)

    def flagged(source, fine_part, coarse_part):
        return jnp.where(source[0].reshape((-1,) + (1,) * (fine_part.ndim - 1)), fine_part, coarse_part)

    ghost2_left = flagged(targets_left, rim_left, inject_side(pick_edge_in(left_edges_one, (0, coarse_one[:, 0, :].shape), targets_left)))
    ghost2_right = flagged(targets_right, rim_right, inject_side(pick_edge_in(right_edges_one, (0, coarse_one[:, 0, :].shape), targets_right)))
    ghost2_low = flagged(targets_low, rim_low, inject_end(pick_edge(places[8], targets_low)))
    ghost2_high = flagged(targets_high, rim_high, inject_end(pick_edge(places[9], targets_high)))
    rate_f2, left_two, right_two, low_two, high_two = jax.vmap(fine_section)(
        fine_one, ghost2_left, ghost2_right, ghost2_low, ghost2_high
    )
    fine_final = 0.5 * (fine_box + fine_one + rate_f2)
    reg_left = pair_mean(0.5 * (left_one + left_two))
    reg_right = pair_mean(0.5 * (right_one + right_two))
    reg_low = pair_mean(0.5 * (low_one + low_two))
    reg_high = pair_mean(0.5 * (high_one + high_two))
    restricted = restrict(fine_final)
    left_regs = shift_x(reg_right, 1)
    right_regs = shift_x(reg_left, -1)
    rows, places = gather_rows((restricted, reg_high, reg_low, left_regs, right_regs))

    def home_pick(place, table_column, block):
        slot_index = slot_of[table_column, block]
        return take_slot(rows, place, slot_index // slot_count, slot_index % slot_count)

    home_mean = home_pick(places[0], column, device_row)
    got_below = home_pick(places[1], column, below_block)
    got_above = home_pick(places[2], column, above_block)
    got_left = home_pick(places[3], column_left, device_row)
    got_right = home_pick(places[4], column_right, device_row)
    face_left = 0.5 * (flux_x1[:, 0] + flux_x2[:, 0])
    face_right = 0.5 * (flux_x1[:, -1] + flux_x2[:, -1])
    face_low = 0.5 * (flux_y1[:, :, 0] + flux_y2[:, :, 0])
    face_high = 0.5 * (flux_y1[:, :, -1] + flux_y2[:, :, -1])
    corr_left = jnp.where(
        refined[column_left, device_row], LAM_COARSE * (got_left - face_left), 0.0
    )
    corr_right = jnp.where(
        refined[column_right, device_row], LAM_COARSE * (face_right - got_right), 0.0
    )
    corr_low = jnp.where(refined[column, below_block], LAM_COARSE * (got_below - face_low), 0.0)
    corr_high = jnp.where(refined[column, above_block], LAM_COARSE * (face_high - got_above), 0.0)
    corr_x = jnp.concatenate(
        [
            corr_left[:, None, :],
            jnp.zeros((3, span_x - 2, span_y), jnp.float32),
            corr_right[:, None, :],
        ],
        axis=1,
    )
    corr_y = jnp.concatenate(
        [
            corr_low[:, :, None],
            jnp.zeros((3, span_x, span_y - 2), jnp.float32),
            corr_high[:, :, None],
        ],
        axis=2,
    )
    coarse_next = coarse_heun + corr_x + corr_y
    coarse_next = jnp.where(refined[column, device_row], home_mean, coarse_next)
    fine_next = jnp.where(is_live[:, None, None, None], fine_final, 0.0)[None]
    return (coarse_next, fine_next)


def solution(mesh):
    in_specs = (P(None, "gx", "gy"), P("gx", "gy", None, None, None), P())
    out_specs = (P(None, "gx", "gy"), P("gx", "gy", None, None, None))
    return jax.shard_map(shards, mesh=mesh, in_specs=in_specs, out_specs=out_specs, check_vma=False)
```

```python
import jax
import jax.numpy as jnp
from jax import lax
from jax.sharding import PartitionSpec as P

LAM_COARSE = 0.2
LAM_FINE = 0.4


def extended(cells, sides, width):
    for axis, dim in sides:
        count = lax.axis_size(axis)
        head = lax.slice_in_dim(cells, 0, width, axis=dim)
        tail = lax.slice_in_dim(cells, cells.shape[dim] - width, cells.shape[dim], axis=dim)
        cells = jnp.concatenate(
            [
                lax.ppermute(tail, axis, [(i, (i + 1) % count) for i in range(count)]),
                cells,
                lax.ppermute(head, axis, [((i + 1) % count, i) for i in range(count)]),
            ],
            axis=dim,
        )
    return cells


def face_flux_x(padded, span_x, span_y):
    cell_minus = padded[:, 0 : span_x + 1, 2 : span_y + 2]
    cell_left = padded[:, 1 : span_x + 2, 2 : span_y + 2]
    cell_right = padded[:, 2 : span_x + 3, 2 : span_y + 2]
    cell_plus = padded[:, 3 : span_x + 4, 2 : span_y + 2]
    face_mean = (7.0 * (cell_left + cell_right) - (cell_minus + cell_plus)) / 12.0
    face_jump = cell_right - cell_left
    return jnp.stack(
        [face_mean[1] - 0.5 * face_jump[0], face_mean[0] - 0.5 * face_jump[1], -0.5 * face_jump[2]]
    )


def face_flux_y(padded, span_x, span_y):
    cell_minus = padded[:, 2 : span_x + 2, 0 : span_y + 1]
    cell_left = padded[:, 2 : span_x + 2, 1 : span_y + 2]
    cell_right = padded[:, 2 : span_x + 2, 2 : span_y + 3]
    cell_plus = padded[:, 2 : span_x + 2, 3 : span_y + 4]
    face_mean = (7.0 * (cell_left + cell_right) - (cell_minus + cell_plus)) / 12.0
    face_jump = cell_right - cell_left
    return jnp.stack(
        [face_mean[2] - 0.5 * face_jump[0], -0.5 * face_jump[1], face_mean[0] - 0.5 * face_jump[2]]
    )


def advance_rate(padded, factor):
    span_x = padded.shape[1] - 4
    span_y = padded.shape[2] - 4
    flux_x = face_flux_x(padded, span_x, span_y)
    flux_y = face_flux_y(padded, span_x, span_y)
    change = -factor * (flux_x[:, 1:] - flux_x[:, :-1] + (flux_y[:, :, 1:] - flux_y[:, :, :-1]))
    return (change, flux_x, flux_y)


def inject_side(coarse_edge):
    doubled = jnp.repeat(coarse_edge, 2, axis=-1)
    return jnp.broadcast_to(doubled[..., None, :], doubled.shape[:-1] + (2, doubled.shape[-1]))


def inject_end(coarse_edge):
    doubled = jnp.repeat(coarse_edge, 2, axis=-1)
    return jnp.broadcast_to(doubled[..., None], doubled.shape + (2,))


def assemble(field, ghost_left, ghost_right, ghost_low, ghost_high):
    middle = jnp.concatenate([ghost_low, field, ghost_high], axis=-1)
    zero_band = jnp.zeros(ghost_left.shape[:-1] + (2,), field.dtype)
    left_full = jnp.concatenate([zero_band, ghost_left, zero_band], axis=-1)
    right_full = jnp.concatenate([zero_band, ghost_right, zero_band], axis=-1)
    return jnp.concatenate([left_full, middle, right_full], axis=-2)


def fine_section(field, ghost_left, ghost_right, ghost_low, ghost_high):
    padded = assemble(field, ghost_left, ghost_right, ghost_low, ghost_high)
    change, flux_x, flux_y = advance_rate(padded, LAM_FINE)
    return (change, flux_x[:, 0], flux_x[:, -1], flux_y[:, :, 0], flux_y[:, :, -1])


def pair_mean(values):
    return 0.5 * (values[..., 0::2] + values[..., 1::2])


def restrict(field):
    paired = field[..., 0::2, :] + field[..., 1::2, :]
    return 0.25 * (paired[..., 0::2] + paired[..., 1::2])


def coarse_margin(field):
    return extended(field, (("gx", 1), ("gy", 2)), 2)


def pick_from(row_index, strips, coarse_edges, targets):
    flag, fine_row, fine_sub, edge_row = targets
    sub_index = jnp.arange(strips.shape[1], dtype=jnp.int32)
    hit_mask = (
        (row_index[None, :, None] == fine_row[:, None, None])
        & (sub_index[None, None, :] == fine_sub[:, None, None])
        & flag[:, None, None]
    )
    fine_part = jnp.sum(
        jnp.where(hit_mask[:, :, :, None, None, None], strips[None], 0.0), axis=(1, 2)
    )
    edge_mask = (row_index[None, :] == edge_row[:, None]) & jnp.logical_not(flag)[:, None]
    edge_part = jnp.sum(jnp.where(edge_mask[:, :, None, None], coarse_edges[None], 0.0), axis=1)
    return (fine_part, edge_part)


def gather_rows(parts):
    flat = jnp.concatenate([part.reshape(-1) for part in parts])
    flat = jnp.pad(flat, (0, -flat.size % 1024))[None]
    rows = lax.all_gather(flat, "gy", axis=0, tiled=True)
    offsets = []
    offset = 0
    for part in parts:
        offsets.append((offset, part.shape))
        offset += part.size
    return rows, offsets


def take_row(rows, place, row):
    offset, shape = place
    size = 1
    for extent in shape:
        size *= extent
    return lax.dynamic_slice(rows, (row, offset), (1, size)).reshape(shape)


def take_slot(rows, place, row, sub):
    offset, shape = place
    size = 1
    for extent in shape[1:]:
        size *= extent
    return lax.dynamic_slice(rows, (row, offset + sub * size), (1, size)).reshape(shape[1:])


def shift_x(values, step):
    count = lax.axis_size("gx")
    return lax.ppermute(values, "gx", [(i, (i + step) % count) for i in range(count)])


def shift_y(values, step):
    count = lax.axis_size("gy")
    return lax.ppermute(values, "gy", [(i, (i + step) % count) for i in range(count)])


def shards(coarse_state, refined_box_state, box_parent):
    count_x = lax.axis_size("gx")
    count_y = lax.axis_size("gy")
    column = lax.axis_index("gx")
    device_row = lax.axis_index("gy")
    slot_count = refined_box_state.shape[1]
    fine_box = refined_box_state[0]
    span_x = coarse_state.shape[1]
    span_y = coarse_state.shape[2]
    block_ids = jnp.arange(count_y, dtype=jnp.int32)
    block_hits = box_parent[:, :, None] == block_ids[None, None, :]
    refined = jnp.any(block_hits, axis=1)
    slot_ids = jnp.arange(box_parent.shape[1], dtype=jnp.int32)
    slot_of = jnp.sum(jnp.where(block_hits, slot_ids[None, :, None], 0), axis=1)
    column_left = (column - 1) % count_x
    column_right = (column + 1) % count_x
    below_block = (device_row - 1) % count_y
    above_block = (device_row + 1) % count_y
    own_table = lax.dynamic_index_in_dim(box_parent, column, 0, keepdims=False)
    own_parents = lax.dynamic_slice_in_dim(own_table, device_row * slot_count, slot_count)
    is_live = own_parents < count_y
    parent = jnp.minimum(own_parents, count_y - 1)

    def fine_source(table_column, block):
        flag = refined[table_column, block]
        slot_index = slot_of[table_column, block]
        return (flag, slot_index // slot_count, slot_index % slot_count, block)

    targets_left = fine_source(column_left, parent)
    targets_right = fine_source(column_right, parent)
    targets_low = fine_source(column, (parent - 1) % count_y)
    targets_high = fine_source(column, (parent + 1) % count_y)
    targets_left_low = fine_source(column_left, (parent - 1) % count_y)
    targets_left_high = fine_source(column_left, (parent + 1) % count_y)
    targets_right_low = fine_source(column_right, (parent - 1) % count_y)
    targets_right_high = fine_source(column_right, (parent + 1) % count_y)

    strip_size = fine_box[:, :, :4, :].size
    right_pack = jnp.concatenate([fine_box[:, :, -4:, :].reshape(-1), coarse_state[:, -2:, :].reshape(-1)])
    left_pack = jnp.concatenate([fine_box[:, :, :4, :].reshape(-1), coarse_state[:, :2, :].reshape(-1)])
    from_left = shift_x(right_pack, 1)
    from_right = shift_x(left_pack, -1)
    strip_shape = fine_box[:, :, :4, :].shape
    rim_shape = coarse_state[:, :2, :].shape
    left_rim = from_left[strip_size:].reshape(rim_shape)
    right_rim = from_right[strip_size:].reshape(rim_shape)

    def coarse_padded(field, ghost_left, ghost_right):
        ghost_low = shift_y(field[:, :, -2:], 1)
        ghost_high = shift_y(field[:, :, :2], -1)
        return assemble(field, ghost_left, ghost_right, ghost_low, ghost_high)

    rate_one, flux_x1, flux_y1 = advance_rate(coarse_padded(coarse_state, left_rim, right_rim), LAM_COARSE)
    coarse_one = coarse_state + rate_one
    one_left = shift_x(coarse_one[:, -2:, :], 1)
    one_right = shift_x(coarse_one[:, :2, :], -1)
    rate_two, flux_x2, flux_y2 = advance_rate(coarse_padded(coarse_one, one_left, one_right), LAM_COARSE)
    coarse_heun = 0.5 * (coarse_state + coarse_one + rate_two)

    parts = (
        from_left[:strip_size].reshape(strip_shape),
        left_rim[:, 1, :],
        from_right[:strip_size].reshape(strip_shape),
        right_rim[:, 0, :],
        fine_box[..., -4:],
        fine_box[..., :4],
        coarse_state[:, :, -1],
        coarse_state[:, :, 0],
        coarse_one[:, :, -1],
        coarse_one[:, :, 0],
        coarse_one[:, -1, :],
        coarse_one[:, 0, :],
    )
    rows, places = gather_rows(parts)
    column_edges_one = lax.slice_in_dim(rows, places[10][0], places[10][0] + 2 * coarse_one[:, 0, :].size, axis=1)
    left_edges_one = shift_x(column_edges_one[:, : coarse_one[:, 0, :].size], 1)
    right_edges_one = shift_x(column_edges_one[:, coarse_one[:, 0, :].size :], -1)

    def pick(place, source):
        flag, fine_row, fine_sub, _ = source
        taken = jnp.stack([take_slot(rows, place, fine_row[s], fine_sub[s]) for s in range(slot_count)])
        return jnp.where(flag.reshape((-1,) + (1,) * (taken.ndim - 1)), taken, 0.0)

    def pick_edge_in(table, place, source):
        flag, _, _, edge_row = source
        taken = jnp.stack([take_row(table, place, edge_row[s]) for s in range(slot_count)])
        return jnp.where(flag.reshape((-1,) + (1,) * (taken.ndim - 1)), 0.0, taken)

    def pick_edge(place, source):
        return pick_edge_in(rows, place, source)

    def corner(place, edge_place, source, row_slice, col_slice, edge_index):
        fine_part = pick(place, source)[:, :, row_slice, col_slice]
        edge_part = pick_edge(edge_place, source)[:, :, edge_index]
        return fine_part + edge_part[:, :, None, None]

    corner_left_low = corner(places[0], places[1], targets_left_low, slice(2, 4), slice(-2, None), -1)
    corner_left_high = corner(places[0], places[1], targets_left_high, slice(2, 4), slice(0, 2), 0)
    corner_right_low = corner(places[2], places[3], targets_right_low, slice(0, 2), slice(-2, None), -1)
    corner_right_high = corner(places[2], places[3], targets_right_high, slice(0, 2), slice(0, 2), 0)

    wide_left = pick(places[0], targets_left)
    wide_right = pick(places[2], targets_right)
    wide_low = pick(places[4], targets_low)
    wide_high = pick(places[5], targets_high)
    ghost_left = wide_left[:, :, 2:, :] + inject_side(pick_edge(places[1], targets_left))
    ghost_right = wide_right[:, :, :2, :] + inject_side(pick_edge(places[3], targets_right))
    ghost_low = wide_low[..., 2:] + inject_end(pick_edge(places[6], targets_low))
    ghost_high = wide_high[..., :2] + inject_end(pick_edge(places[7], targets_high))
    rate_f1, left_one, right_one, low_one, high_one = jax.vmap(fine_section)(
        fine_box, ghost_left, ghost_right, ghost_low, ghost_high
    )
    fine_one = fine_box + rate_f1

    def rim_rate(padded):
        return advance_rate(padded, LAM_FINE)[0]

    zero_pair = jnp.zeros(fine_box.shape[:2] + (2, 2), jnp.float32)

    def rows_of(low_end, middle, high_end):
        return jnp.concatenate([low_end, middle, high_end], axis=3)

    def cols_of(low_end, middle, high_end):
        return jnp.concatenate([low_end, middle, high_end], axis=2)

    padded_left = jnp.concatenate(
        [
            rows_of(zero_pair, wide_left[:, :, :2, :], zero_pair),
            rows_of(corner_left_low, wide_left[:, :, 2:, :], corner_left_high),
            rows_of(zero_pair, fine_box[:, :, :2, :], zero_pair),
        ],
        axis=2,
    )
    padded_right = jnp.concatenate(
        [
            rows_of(zero_pair, fine_box[:, :, -2:, :], zero_pair),
            rows_of(corner_right_low, wide_right[:, :, :2, :], corner_right_high),
            rows_of(zero_pair, wide_right[:, :, 2:, :], zero_pair),
        ],
        axis=2,
    )
    padded_low = jnp.concatenate(
        [
            cols_of(zero_pair, wide_low[..., :2], zero_pair),
            cols_of(corner_left_low, wide_low[..., 2:], corner_right_low),
            cols_of(zero_pair, fine_box[..., :2], zero_pair),
        ],
        axis=3,
    )
    padded_high = jnp.concatenate(
        [
            cols_of(zero_pair, fine_box[..., -2:], zero_pair),
            cols_of(corner_left_high, wide_high[..., :2], corner_right_high),
            cols_of(zero_pair, wide_high[..., 2:], zero_pair),
        ],
        axis=3,
    )
    rim_left = wide_left[:, :, 2:, :] + jax.vmap(rim_rate)(padded_left)
    rim_right = wide_right[:, :, :2, :] + jax.vmap(rim_rate)(padded_right)
    rim_low = wide_low[..., 2:] + jax.vmap(rim_rate)(padded_low)
    rim_high = wide_high[..., :2] + jax.vmap(rim_rate)(padded_high)

    def flagged(source, fine_part, coarse_part):
        return jnp.where(source[0].reshape((-1,) + (1,) * (fine_part.ndim - 1)), fine_part, coarse_part)

    ghost2_left = flagged(targets_left, rim_left, inject_side(pick_edge_in(left_edges_one, (0, coarse_one[:, 0, :].shape), targets_left)))
    ghost2_right = flagged(targets_right, rim_right, inject_side(pick_edge_in(right_edges_one, (0, coarse_one[:, 0, :].shape), targets_right)))
    ghost2_low = flagged(targets_low, rim_low, inject_end(pick_edge(places[8], targets_low)))
    ghost2_high = flagged(targets_high, rim_high, inject_end(pick_edge(places[9], targets_high)))
    rate_f2, left_two, right_two, low_two, high_two = jax.vmap(fine_section)(
        fine_one, ghost2_left, ghost2_right, ghost2_low, ghost2_high
    )
    fine_final = 0.5 * (fine_box + fine_one + rate_f2)
    reg_left = pair_mean(0.5 * (left_one + left_two))
    reg_right = pair_mean(0.5 * (right_one + right_two))
    reg_low = pair_mean(0.5 * (low_one + low_two))
    reg_high = pair_mean(0.5 * (high_one + high_two))
    restricted = restrict(fine_final)
    rows, places = gather_rows((restricted, reg_high, reg_low, reg_right, reg_left))

    def home_pick(place, table_column, block):
        slot_index = slot_of[table_column, block]
        return take_slot(rows, place, slot_index // slot_count, slot_index % slot_count)

    home_mean = home_pick(places[0], column, device_row)
    got_below = home_pick(places[1], column, below_block)
    got_above = home_pick(places[2], column, above_block)
    got_left = shift_x(home_pick(places[3], column, device_row), 1)
    got_right = shift_x(home_pick(places[4], column, device_row), -1)
    face_left = 0.5 * (flux_x1[:, 0] + flux_x2[:, 0])
    face_right = 0.5 * (flux_x1[:, -1] + flux_x2[:, -1])
    face_low = 0.5 * (flux_y1[:, :, 0] + flux_y2[:, :, 0])
    face_high = 0.5 * (flux_y1[:, :, -1] + flux_y2[:, :, -1])
    corr_left = jnp.where(
        refined[column_left, device_row], LAM_COARSE * (got_left - face_left), 0.0
    )
    corr_right = jnp.where(
        refined[column_right, device_row], LAM_COARSE * (face_right - got_right), 0.0
    )
    corr_low = jnp.where(refined[column, below_block], LAM_COARSE * (got_below - face_low), 0.0)
    corr_high = jnp.where(refined[column, above_block], LAM_COARSE * (face_high - got_above), 0.0)
    corr_x = jnp.concatenate(
        [
            corr_left[:, None, :],
            jnp.zeros((3, span_x - 2, span_y), jnp.float32),
            corr_right[:, None, :],
        ],
        axis=1,
    )
    corr_y = jnp.concatenate(
        [
            corr_low[:, :, None],
            jnp.zeros((3, span_x, span_y - 2), jnp.float32),
            corr_high[:, :, None],
        ],
        axis=2,
    )
    coarse_next = coarse_heun + corr_x + corr_y
    coarse_next = jnp.where(refined[column, device_row], home_mean, coarse_next)
    fine_next = jnp.where(is_live[:, None, None, None], fine_final, 0.0)[None]
    return (coarse_next, fine_next)


def solution(mesh):
    in_specs = (P(None, "gx", "gy"), P("gx", "gy", None, None, None), P())
    out_specs = (P(None, "gx", "gy"), P("gx", "gy", None, None, None))
    return jax.shard_map(shards, mesh=mesh, in_specs=in_specs, out_specs=out_specs, check_vma=False)
```

```python
import jax
import jax.numpy as jnp
from jax import lax
from jax.sharding import PartitionSpec as P

LAM_COARSE = 0.2
LAM_FINE = 0.4


def extended(cells, sides, width):
    for axis, dim in sides:
        count = lax.axis_size(axis)
        head = lax.slice_in_dim(cells, 0, width, axis=dim)
        tail = lax.slice_in_dim(cells, cells.shape[dim] - width, cells.shape[dim], axis=dim)
        cells = jnp.concatenate(
            [
                lax.ppermute(tail, axis, [(i, (i + 1) % count) for i in range(count)]),
                cells,
                lax.ppermute(head, axis, [((i + 1) % count, i) for i in range(count)]),
            ],
            axis=dim,
        )
    return cells


def face_flux_x(padded, span_x, span_y):
    cell_minus = padded[:, 0 : span_x + 1, 2 : span_y + 2]
    cell_left = padded[:, 1 : span_x + 2, 2 : span_y + 2]
    cell_right = padded[:, 2 : span_x + 3, 2 : span_y + 2]
    cell_plus = padded[:, 3 : span_x + 4, 2 : span_y + 2]
    face_mean = (7.0 * (cell_left + cell_right) - (cell_minus + cell_plus)) / 12.0
    face_jump = cell_right - cell_left
    return jnp.stack(
        [face_mean[1] - 0.5 * face_jump[0], face_mean[0] - 0.5 * face_jump[1], -0.5 * face_jump[2]]
    )


def face_flux_y(padded, span_x, span_y):
    cell_minus = padded[:, 2 : span_x + 2, 0 : span_y + 1]
    cell_left = padded[:, 2 : span_x + 2, 1 : span_y + 2]
    cell_right = padded[:, 2 : span_x + 2, 2 : span_y + 3]
    cell_plus = padded[:, 2 : span_x + 2, 3 : span_y + 4]
    face_mean = (7.0 * (cell_left + cell_right) - (cell_minus + cell_plus)) / 12.0
    face_jump = cell_right - cell_left
    return jnp.stack(
        [face_mean[2] - 0.5 * face_jump[0], -0.5 * face_jump[1], face_mean[0] - 0.5 * face_jump[2]]
    )


def advance_rate(padded, factor):
    span_x = padded.shape[1] - 4
    span_y = padded.shape[2] - 4
    flux_x = face_flux_x(padded, span_x, span_y)
    flux_y = face_flux_y(padded, span_x, span_y)
    change = -factor * (flux_x[:, 1:] - flux_x[:, :-1] + (flux_y[:, :, 1:] - flux_y[:, :, :-1]))
    return (change, flux_x, flux_y)


def inject_side(coarse_edge):
    doubled = jnp.repeat(coarse_edge, 2, axis=-1)
    return jnp.broadcast_to(doubled[..., None, :], doubled.shape[:-1] + (2, doubled.shape[-1]))


def inject_end(coarse_edge):
    doubled = jnp.repeat(coarse_edge, 2, axis=-1)
    return jnp.broadcast_to(doubled[..., None], doubled.shape + (2,))


def assemble(field, ghost_left, ghost_right, ghost_low, ghost_high):
    middle = jnp.concatenate([ghost_low, field, ghost_high], axis=-1)
    zero_band = jnp.zeros(ghost_left.shape[:-1] + (2,), field.dtype)
    left_full = jnp.concatenate([zero_band, ghost_left, zero_band], axis=-1)
    right_full = jnp.concatenate([zero_band, ghost_right, zero_band], axis=-1)
    return jnp.concatenate([left_full, middle, right_full], axis=-2)


def fine_section(field, ghost_left, ghost_right, ghost_low, ghost_high):
    padded = assemble(field, ghost_left, ghost_right, ghost_low, ghost_high)
    change, flux_x, flux_y = advance_rate(padded, LAM_FINE)
    return (change, flux_x[:, 0], flux_x[:, -1], flux_y[:, :, 0], flux_y[:, :, -1])


def pair_mean(values):
    return 0.5 * (values[..., 0::2] + values[..., 1::2])


def restrict(field):
    paired = field[..., 0::2, :] + field[..., 1::2, :]
    return 0.25 * (paired[..., 0::2] + paired[..., 1::2])


def coarse_margin(field):
    return extended(field, (("gx", 1), ("gy", 2)), 2)


def pick_from(row_index, strips, coarse_edges, targets):
    flag, fine_row, fine_sub, edge_row = targets
    sub_index = jnp.arange(strips.shape[1], dtype=jnp.int32)
    hit_mask = (
        (row_index[None, :, None] == fine_row[:, None, None])
        & (sub_index[None, None, :] == fine_sub[:, None, None])
        & flag[:, None, None]
    )
    fine_part = jnp.sum(
        jnp.where(hit_mask[:, :, :, None, None, None], strips[None], 0.0), axis=(1, 2)
    )
    edge_mask = (row_index[None, :] == edge_row[:, None]) & jnp.logical_not(flag)[:, None]
    edge_part = jnp.sum(jnp.where(edge_mask[:, :, None, None], coarse_edges[None], 0.0), axis=1)
    return (fine_part, edge_part)


def gather_rows(parts):
    flat = jnp.concatenate([part.reshape(-1) for part in parts])
    flat = jnp.pad(flat, (0, -flat.size % 1024))[None]
    rows = lax.all_gather(flat, "gy", axis=0, tiled=True)
    offsets = []
    offset = 0
    for part in parts:
        offsets.append((offset, part.shape))
        offset += part.size
    return rows, offsets


def take_row(rows, place, row):
    offset, shape = place
    size = 1
    for extent in shape:
        size *= extent
    return lax.dynamic_slice(rows, (row, offset), (1, size)).reshape(shape)


def take_slot(rows, place, row, sub):
    offset, shape = place
    size = 1
    for extent in shape[1:]:
        size *= extent
    return lax.dynamic_slice(rows, (row, offset + sub * size), (1, size)).reshape(shape[1:])


def shift_x(values, step):
    count = lax.axis_size("gx")
    return lax.ppermute(values, "gx", [(i, (i + step) % count) for i in range(count)])


def shift_y(values, step):
    count = lax.axis_size("gy")
    return lax.ppermute(values, "gy", [(i, (i + step) % count) for i in range(count)])


def shards(coarse_state, refined_box_state, box_parent):
    count_x = lax.axis_size("gx")
    count_y = lax.axis_size("gy")
    column = lax.axis_index("gx")
    device_row = lax.axis_index("gy")
    slot_count = refined_box_state.shape[1]
    fine_box = refined_box_state[0]
    span_x = coarse_state.shape[1]
    span_y = coarse_state.shape[2]
    block_ids = jnp.arange(count_y, dtype=jnp.int32)
    block_hits = box_parent[:, :, None] == block_ids[None, None, :]
    refined = jnp.any(block_hits, axis=1)
    slot_ids = jnp.arange(box_parent.shape[1], dtype=jnp.int32)
    slot_of = jnp.sum(jnp.where(block_hits, slot_ids[None, :, None], 0), axis=1)
    column_left = (column - 1) % count_x
    column_right = (column + 1) % count_x
    below_block = (device_row - 1) % count_y
    above_block = (device_row + 1) % count_y
    own_table = lax.dynamic_index_in_dim(box_parent, column, 0, keepdims=False)
    own_parents = lax.dynamic_slice_in_dim(own_table, device_row * slot_count, slot_count)
    is_live = own_parents < count_y
    parent = jnp.minimum(own_parents, count_y - 1)

    def fine_source(table_column, block):
        flag = refined[table_column, block]
        slot_index = slot_of[table_column, block]
        return (flag, slot_index // slot_count, slot_index % slot_count, block)

    targets_left = fine_source(column_left, parent)
    targets_right = fine_source(column_right, parent)
    targets_low = fine_source(column, (parent - 1) % count_y)
    targets_high = fine_source(column, (parent + 1) % count_y)
    targets_left_low = fine_source(column_left, (parent - 1) % count_y)
    targets_left_high = fine_source(column_left, (parent + 1) % count_y)
    targets_right_low = fine_source(column_right, (parent - 1) % count_y)
    targets_right_high = fine_source(column_right, (parent + 1) % count_y)

    strip_size = fine_box[:, :, :4, :].size
    right_pack = jnp.concatenate([fine_box[:, :, -4:, :].reshape(-1), coarse_state[:, -2:, :].reshape(-1)])
    left_pack = jnp.concatenate([fine_box[:, :, :4, :].reshape(-1), coarse_state[:, :2, :].reshape(-1)])
    from_left = shift_x(right_pack, 1)
    from_right = shift_x(left_pack, -1)
    strip_shape = fine_box[:, :, :4, :].shape
    rim_shape = coarse_state[:, :2, :].shape
    left_rim = from_left[strip_size:].reshape(rim_shape)
    right_rim = from_right[strip_size:].reshape(rim_shape)

    def coarse_padded(field, ghost_left, ghost_right):
        ghost_low = shift_y(field[:, :, -2:], 1)
        ghost_high = shift_y(field[:, :, :2], -1)
        return assemble(field, ghost_left, ghost_right, ghost_low, ghost_high)

    rate_one, flux_x1, flux_y1 = advance_rate(coarse_padded(coarse_state, left_rim, right_rim), LAM_COARSE)
    coarse_one = coarse_state + rate_one
    one_left = shift_x(coarse_one[:, -2:, :], 1)
    one_right = shift_x(coarse_one[:, :2, :], -1)
    rate_two, flux_x2, flux_y2 = advance_rate(coarse_padded(coarse_one, one_left, one_right), LAM_COARSE)
    coarse_heun = 0.5 * (coarse_state + coarse_one + rate_two)

    parts = (
        from_left[:strip_size].reshape(strip_shape),
        left_rim[:, 1, :],
        from_right[:strip_size].reshape(strip_shape),
        right_rim[:, 0, :],
        fine_box[..., -4:],
        fine_box[..., :4],
        coarse_state[:, :, -1],
        coarse_state[:, :, 0],
        coarse_one[:, :, -1],
        coarse_one[:, :, 0],
        coarse_one[:, -1, :],
        coarse_one[:, 0, :],
    )
    rows, places = gather_rows(parts)
    column_edges_one = lax.slice_in_dim(rows, places[10][0], places[10][0] + 2 * coarse_one[:, 0, :].size, axis=1)
    left_edges_one = shift_x(column_edges_one[:, : coarse_one[:, 0, :].size], 1)
    right_edges_one = shift_x(column_edges_one[:, coarse_one[:, 0, :].size :], -1)

    def pick(place, source):
        flag, fine_row, fine_sub, _ = source
        taken = jnp.stack([take_slot(rows, place, fine_row[s], fine_sub[s]) for s in range(slot_count)])
        return jnp.where(flag.reshape((-1,) + (1,) * (taken.ndim - 1)), taken, 0.0)

    def pick_edge_in(table, place, source):
        flag, _, _, edge_row = source
        taken = jnp.stack([take_row(table, place, edge_row[s]) for s in range(slot_count)])
        return jnp.where(flag.reshape((-1,) + (1,) * (taken.ndim - 1)), 0.0, taken)

    def pick_edge(place, source):
        return pick_edge_in(rows, place, source)

    def corner(place, edge_place, source, row_slice, col_slice, edge_index):
        fine_part = pick(place, source)[:, :, row_slice, col_slice]
        edge_part = pick_edge(edge_place, source)[:, :, edge_index]
        return fine_part + edge_part[:, :, None, None]

    corner_left_low = corner(places[0], places[1], targets_left_low, slice(2, 4), slice(-2, None), -1)
    corner_left_high = corner(places[0], places[1], targets_left_high, slice(2, 4), slice(0, 2), 0)
    corner_right_low = corner(places[2], places[3], targets_right_low, slice(0, 2), slice(-2, None), -1)
    corner_right_high = corner(places[2], places[3], targets_right_high, slice(0, 2), slice(0, 2), 0)

    wide_left = pick(places[0], targets_left)
    wide_right = pick(places[2], targets_right)
    wide_low = pick(places[4], targets_low)
    wide_high = pick(places[5], targets_high)
    ghost_left = wide_left[:, :, 2:, :] + inject_side(pick_edge(places[1], targets_left))
    ghost_right = wide_right[:, :, :2, :] + inject_side(pick_edge(places[3], targets_right))
    ghost_low = wide_low[..., 2:] + inject_end(pick_edge(places[6], targets_low))
    ghost_high = wide_high[..., :2] + inject_end(pick_edge(places[7], targets_high))
    rate_f1, left_one, right_one, low_one, high_one = jax.vmap(fine_section)(
        fine_box, ghost_left, ghost_right, ghost_low, ghost_high
    )
    fine_one = fine_box + rate_f1

    def rim_rate(padded):
        return advance_rate(padded, LAM_FINE)[0]

    zero_pair = jnp.zeros(fine_box.shape[:2] + (2, 2), jnp.float32)

    def rows_of(low_end, middle, high_end):
        return jnp.concatenate([low_end, middle, high_end], axis=3)

    def cols_of(low_end, middle, high_end):
        return jnp.concatenate([low_end, middle, high_end], axis=2)

    padded_left = jnp.concatenate(
        [
            rows_of(zero_pair, wide_left[:, :, :2, :], zero_pair),
            rows_of(corner_left_low, wide_left[:, :, 2:, :], corner_left_high),
            rows_of(zero_pair, fine_box[:, :, :2, :], zero_pair),
        ],
        axis=2,
    )
    padded_right = jnp.concatenate(
        [
            rows_of(zero_pair, fine_box[:, :, -2:, :], zero_pair),
            rows_of(corner_right_low, wide_right[:, :, :2, :], corner_right_high),
            rows_of(zero_pair, wide_right[:, :, 2:, :], zero_pair),
        ],
        axis=2,
    )
    padded_low = jnp.concatenate(
        [
            cols_of(zero_pair, wide_low[..., :2], zero_pair),
            cols_of(corner_left_low, wide_low[..., 2:], corner_right_low),
            cols_of(zero_pair, fine_box[..., :2], zero_pair),
        ],
        axis=3,
    )
    padded_high = jnp.concatenate(
        [
            cols_of(zero_pair, fine_box[..., -2:], zero_pair),
            cols_of(corner_left_high, wide_high[..., :2], corner_right_high),
            cols_of(zero_pair, wide_high[..., 2:], zero_pair),
        ],
        axis=3,
    )
    rim_left = wide_left[:, :, 2:, :] + jax.vmap(rim_rate)(padded_left)
    rim_right = wide_right[:, :, :2, :] + jax.vmap(rim_rate)(padded_right)
    rim_low = wide_low[..., 2:] + jax.vmap(rim_rate)(padded_low)
    rim_high = wide_high[..., :2] + jax.vmap(rim_rate)(padded_high)

    def flagged(source, fine_part, coarse_part):
        return jnp.where(source[0].reshape((-1,) + (1,) * (fine_part.ndim - 1)), fine_part, coarse_part)

    ghost2_left = flagged(targets_left, rim_left, inject_side(pick_edge_in(left_edges_one, (0, coarse_one[:, 0, :].shape), targets_left)))
    ghost2_right = flagged(targets_right, rim_right, inject_side(pick_edge_in(right_edges_one, (0, coarse_one[:, 0, :].shape), targets_right)))
    ghost2_low = flagged(targets_low, rim_low, inject_end(pick_edge(places[8], targets_low)))
    ghost2_high = flagged(targets_high, rim_high, inject_end(pick_edge(places[9], targets_high)))
    rate_f2, left_two, right_two, low_two, high_two = jax.vmap(fine_section)(
        fine_one, ghost2_left, ghost2_right, ghost2_low, ghost2_high
    )
    fine_final = 0.5 * (fine_box + fine_one + rate_f2)
    reg_left = pair_mean(0.5 * (left_one + left_two))
    reg_right = pair_mean(0.5 * (right_one + right_two))
    reg_low = pair_mean(0.5 * (low_one + low_two))
    reg_high = pair_mean(0.5 * (high_one + high_two))
    restricted = restrict(fine_final)
    rows, places = gather_rows((restricted, reg_high, reg_low, reg_right, reg_left))

    def home_pick(place, table_column, block):
        slot_index = slot_of[table_column, block]
        return take_slot(rows, place, slot_index // slot_count, slot_index % slot_count)

    home_mean = home_pick(places[0], column, device_row)
    got_below = home_pick(places[1], column, below_block)
    got_above = home_pick(places[2], column, above_block)
    got_left = shift_x(home_pick(places[3], column, device_row), 1)
    got_right = shift_x(home_pick(places[4], column, device_row), -1)
    face_left = 0.5 * (flux_x1[:, 0] + flux_x2[:, 0])
    face_right = 0.5 * (flux_x1[:, -1] + flux_x2[:, -1])
    face_low = 0.5 * (flux_y1[:, :, 0] + flux_y2[:, :, 0])
    face_high = 0.5 * (flux_y1[:, :, -1] + flux_y2[:, :, -1])
    corr_left = jnp.where(
        refined[column_left, device_row], LAM_COARSE * (got_left - face_left), 0.0
    )
    corr_right = jnp.where(
        refined[column_right, device_row], LAM_COARSE * (face_right - got_right), 0.0
    )
    corr_low = jnp.where(refined[column, below_block], LAM_COARSE * (got_below - face_low), 0.0)
    corr_high = jnp.where(refined[column, above_block], LAM_COARSE * (face_high - got_above), 0.0)
    row_ids = jnp.arange(span_x, dtype=jnp.int32)[None, :, None]
    col_ids = jnp.arange(span_y, dtype=jnp.int32)[None, None, :]
    corr_x = jnp.where(row_ids == 0, corr_left[:, None, :], jnp.where(row_ids == span_x - 1, corr_right[:, None, :], 0.0))
    corr_y = jnp.where(col_ids == 0, corr_low[:, :, None], jnp.where(col_ids == span_y - 1, corr_high[:, :, None], 0.0))
    coarse_next = coarse_heun + corr_x + corr_y
    coarse_next = jnp.where(refined[column, device_row], home_mean, coarse_next)
    fine_next = jnp.where(is_live[:, None, None, None], fine_final, 0.0)[None]
    return (coarse_next, fine_next)


def solution(mesh):
    in_specs = (P(None, "gx", "gy"), P("gx", "gy", None, None, None), P())
    out_specs = (P(None, "gx", "gy"), P("gx", "gy", None, None, None))
    return jax.shard_map(shards, mesh=mesh, in_specs=in_specs, out_specs=out_specs, check_vma=False)
```
